128 devices in a mesh: entry: 4 (over y_hi, core), fft: 32 (over y_lo, z, x).
Axes of the slice: x: 4, y: 4 (y_hi: 2, y_lo: 2; y = y_hi * 2 + y_lo), z: 4, core: 2. Of those that a mesh axis runs over, the one named last changes fastest.
Arguments:
- left_zero_zero: int32 [2048, 4096], P('entry', 'fft'), may hold values from 0 to 65535
- left_zero_one: int32 [2048, 4096], P('entry', 'fft'), may hold values from 0 to 65535
- left_one_zero: int32 [2048, 4096], P('entry', 'fft'), may hold values from 0 to 65535
- left_one_one: int32 [2048, 4096], P('entry', 'fft'), may hold values from 0 to 65535
- right_zero_zero: int32 [2048, 4096], P('entry', 'fft'), may hold values from 0 to 65535
- right_zero_one: int32 [2048, 4096], P('entry', 'fft'), may hold values from 0 to 65535
- right_one_zero: int32 [2048, 4096], P('entry', 'fft'), may hold values from 0 to 65535
- right_one_one: int32 [2048, 4096], P('entry', 'fft'), may hold values from 0 to 65535
Outputs:
- product: float32 [4, 4096, 4096], P('entry', None, 'fft')
The draws below stay inside these ranges and needn't reach their ends.
All inputs are finite; a program needn't handle non-finite values.
Results may differ from the reference program's by a relative error of at most 0.0001.
Values sent between devices are 32-bit elements; how exact they have to be, the bound alone decides.
No kernel may reach another device: no remote copies, remote signals or barrier semaphores. Data moves between devices by JAX's collectives and lax.ppermute only.
A program may use at most 128 MiB of HBM per device.

```python
import math
import jax
import jax.numpy as jnp

ROWS = 4096
COLS = 4096
HALF = 2048


def place_ends(drawn, own_key, least, top_value):
    index_at = [jax.random.randint(jax.random.fold_in(own_key, axis), (), 0, length) for axis, length in enumerate(drawn.shape)]
    main_axis = drawn.shape.index(max(drawn.shape))
    beside = index_at[:main_axis] + [(index_at[main_axis] + 1) % drawn.shape[main_axis]] + index_at[main_axis + 1:]
    return drawn.at[tuple(index_at)].set(least).at[tuple(beside)].set(top_value)


def setup_inputs(seed: int = 0) -> dict:
    arg_keys = jax.random.split(jax.random.key(seed), 9)
    left_zero_zero = place_ends(jax.random.randint(arg_keys[0], (HALF, COLS), 0, 65536), jax.random.fold_in(arg_keys[0], 1), 0, 65535).astype(jnp.int32)
    left_zero_one = place_ends(jax.random.randint(arg_keys[1], (HALF, COLS), 0, 65536), jax.random.fold_in(arg_keys[1], 1), 0, 65535).astype(jnp.int32)
    left_one_zero = place_ends(jax.random.randint(arg_keys[2], (HALF, COLS), 0, 65536), jax.random.fold_in(arg_keys[2], 1), 0, 65535).astype(jnp.int32)
    left_one_one = place_ends(jax.random.randint(arg_keys[3], (HALF, COLS), 0, 65536), jax.random.fold_in(arg_keys[3], 1), 0, 65535).astype(jnp.int32)
    right_zero_zero = place_ends(jax.random.randint(arg_keys[4], (HALF, COLS), 0, 65536), jax.random.fold_in(arg_keys[4], 1), 0, 65535).astype(jnp.int32)
    right_zero_one = place_ends(jax.random.randint(arg_keys[5], (HALF, COLS), 0, 65536), jax.random.fold_in(arg_keys[5], 1), 0, 65535).astype(jnp.int32)
    right_one_zero = place_ends(jax.random.randint(arg_keys[6], (HALF, COLS), 0, 65536), jax.random.fold_in(arg_keys[6], 1), 0, 65535).astype(jnp.int32)
    right_one_one = place_ends(jax.random.randint(arg_keys[7], (HALF, COLS), 0, 65536), jax.random.fold_in(arg_keys[7], 1), 0, 65535).astype(jnp.int32)
    return dict(left_zero_zero=left_zero_zero, left_zero_one=left_zero_one, left_one_zero=left_one_zero, left_one_one=left_one_one, right_zero_zero=right_zero_zero, right_zero_one=right_zero_one, right_one_zero=right_one_zero, right_one_one=right_one_one)


def spectrum(limbs, length):
    values = (limbs.astype(jnp.float32) - 32768.0) * (1.0 / 32768.0)
    return jnp.fft.rfft(values.reshape(-1), n=length)

def reference(left_zero_zero, left_zero_one, left_one_zero, left_one_one, right_zero_zero, right_zero_one, right_one_zero, right_one_one):
    length = ROWS * COLS
    lefts = ((spectrum(left_zero_zero, length), spectrum(left_zero_one, length)), (spectrum(left_one_zero, length), spectrum(left_one_one, length)))
    rights = ((spectrum(right_zero_zero, length), spectrum(right_zero_one, length)), (spectrum(right_one_zero, length), spectrum(right_one_one, length)))
    out_scale = 1.0 / math.sqrt(HALF * COLS)
    results = []
    for upper_pick in range(2):
        for lower_pick in range(2):
            mixed = lefts[upper_pick][0] * rights[0][lower_pick] + lefts[upper_pick][1] * rights[1][lower_pick]
            results.append(jnp.fft.irfft(mixed, n=length) * out_scale)
    return jnp.stack(results).reshape(4, ROWS, COLS)
```

```python
import math

import jax
import jax.numpy as jnp
from jax import lax
from jax.sharding import PartitionSpec as P

RADIX = 64


exact_precision = lax.Precision.HIGHEST


def contract(pattern, left_op, right_op):
    return jnp.einsum(
        pattern, left_op, right_op, precision=exact_precision, preferred_element_type=jnp.float32
    )


def iota(count):
    return jnp.arange(count, dtype=jnp.int32)


def angle_table(first_part, second_part, length, sense_sign):
    turns = first_part[:, None] * second_part[None, :] % length
    phase_angle = turns.astype(jnp.float32) * (2.0 * math.pi / length)
    return (jnp.cos(phase_angle), sense_sign * jnp.sin(phase_angle))


def rotate(real_part, imag_part, cosine, sine):
    return (real_part * cosine - imag_part * sine, real_part * sine + imag_part * cosine)


def complex_product(left_real, left_imag, right_real, right_imag):
    return (
        left_real * right_real - left_imag * right_imag,
        left_real * right_imag + left_imag * right_real,
    )


def table_left(pattern, table, real_part, imag_part):
    cosine, sine = table
    if imag_part is None:
        return contract(pattern, cosine, real_part), contract(pattern, sine, real_part)
    return (
        contract(pattern, cosine, real_part) - contract(pattern, sine, imag_part),
        contract(pattern, sine, real_part) + contract(pattern, cosine, imag_part),
    )


def table_right(pattern, real_part, imag_part, table):
    cosine, sine = table
    return (
        contract(pattern, real_part, cosine) - contract(pattern, imag_part, sine),
        contract(pattern, real_part, sine) + contract(pattern, imag_part, cosine),
    )


def digits(limbs):
    return (limbs.astype(jnp.float32) - 32768.0) * (1.0 / 32768.0)


def column_half(values):
    row_count, column_count = values.shape
    length = 2 * row_count
    inner_size = length // RADIX
    outer_count = row_count // inner_size
    first = angle_table(iota(RADIX), iota(outer_count), RADIX, -1.0)
    flat = values.reshape(outer_count, inner_size * column_count)
    step_real, step_imag = table_left("ja,an->jn", first, flat, None)
    step_real = step_real.reshape(RADIX, inner_size, column_count)
    step_imag = step_imag.reshape(RADIX, inner_size, column_count)
    twist_cos, twist_sin = angle_table(iota(RADIX), iota(inner_size), length, -1.0)
    step_real, step_imag = rotate(
        step_real, step_imag, twist_cos[:, :, None], twist_sin[:, :, None]
    )
    second = angle_table(iota(inner_size // 2), iota(inner_size), inner_size, -1.0)
    final_real, final_imag = table_left("mb,jbc->mjc", second, step_real, step_imag)
    alternating = (1 - 2 * (iota(inner_size) % 2)).astype(jnp.float32)
    nyquist = contract("b,bc->c", alternating, step_real[0])
    final_imag = final_imag.at[0, 0].set(nyquist)
    return final_real, final_imag


def column_transform(real_part, imag_part, length, sense_sign):
    inner_size = length // RADIX
    outer_count = real_part.shape[0] // inner_size
    column_count = real_part.shape[1]
    first = angle_table(iota(RADIX), iota(outer_count), RADIX, sense_sign)
    flat_real = real_part.reshape(outer_count, inner_size * column_count)
    flat_imag = imag_part.reshape(outer_count, inner_size * column_count)
    step_real, step_imag = table_left("ja,an->jn", first, flat_real, flat_imag)
    step_real = step_real.reshape(RADIX, inner_size, column_count)
    step_imag = step_imag.reshape(RADIX, inner_size, column_count)
    twist_cos, twist_sin = angle_table(iota(RADIX), iota(inner_size), length, sense_sign)
    step_real, step_imag = rotate(
        step_real, step_imag, twist_cos[:, :, None], twist_sin[:, :, None]
    )
    second_cos, second_sin = angle_table(iota(inner_size), iota(inner_size), inner_size, sense_sign)
    final_real = contract("mb,kbc->mkc", second_cos, step_real) - contract(
        "mb,kbc->mkc", second_sin, step_imag
    )
    return final_real.reshape(length, column_count)


def row_forward(real_part, imag_part, sense_sign):
    source_count, _, column_count = real_part.shape
    length = source_count * column_count
    first = angle_table(iota(source_count), iota(source_count), source_count, sense_sign)
    step_real, step_imag = table_left("us,src->urc", first, real_part, imag_part)
    twist_cos, twist_sin = angle_table(iota(source_count), iota(column_count), length, sense_sign)
    step_real, step_imag = rotate(
        step_real, step_imag, twist_cos[:, None, :], twist_sin[:, None, :]
    )
    second = angle_table(iota(column_count), iota(column_count), column_count, sense_sign)
    return table_right("urc,cv->urv", step_real, step_imag, second)


def row_inverse(real_part, imag_part, sense_sign):
    source_count, _, column_count = real_part.shape
    length = source_count * column_count
    second = angle_table(iota(column_count), iota(column_count), column_count, sense_sign)
    step_real, step_imag = table_right("urv,vc->urc", real_part, imag_part, second)
    twist_cos, twist_sin = angle_table(iota(source_count), iota(column_count), length, sense_sign)
    step_real, step_imag = rotate(
        step_real, step_imag, twist_cos[:, None, :], twist_sin[:, None, :]
    )
    first = angle_table(iota(source_count), iota(source_count), source_count, sense_sign)
    return table_left("su,urc->src", first, step_real, step_imag)


def local(
    left_zero_zero,
    left_zero_one,
    left_one_zero,
    left_one_one,
    right_zero_zero,
    right_zero_one,
    right_one_zero,
    right_one_one,
):
    lefts = [[left_zero_zero, left_zero_one], [left_one_zero, left_one_one]]
    rights = [[right_zero_zero, right_zero_one], [right_one_zero, right_one_one]]
    entry_count = lax.axis_size("entry")
    fft_count = lax.axis_size("fft")
    fft_place = lax.axis_index("fft")
    on_first = fft_place == 0
    local_cols = left_zero_zero.shape[1]
    row_count = left_zero_zero.shape[0] * entry_count
    length = 2 * row_count * local_cols * fft_count
    column_count = local_cols * fft_count
    rows_here = 2 * row_count // (2 * fft_count)

    held_k1 = jnp.concatenate(
        [fft_place * rows_here + iota(rows_here), jnp.full((1,), row_count, jnp.int32)]
    )
    source_cols = (iota(fft_count)[:, None] * local_cols + iota(local_cols)[None, :])
    turns = source_cols[:, None, :] * held_k1[None, :, None] % length
    big_angle = turns.astype(jnp.float32) * (2.0 * math.pi / length)
    big_cos = jnp.cos(big_angle)
    big_sin = jnp.sin(big_angle)

    spectra = []
    for member in range(4):
        if member < 2:
            pieces = [lefts[target // 2][member] for target in range(4)]
        else:
            pieces = [rights[member - 2][target % 2] for target in range(4)]
        outgoing = digits(jnp.stack(pieces))
        arrived = lax.all_to_all(outgoing, "entry", 0, 0, tiled=True)
        arrived = arrived.reshape(row_count, local_cols)
        half_real, half_imag = column_half(arrived)
        payload = jnp.stack([half_real, half_imag], axis=1)
        got = lax.all_to_all(payload, "fft", 0, 0, tiled=True)
        got_real = got[:, 0]
        got_imag = got[:, 1]
        packed = got_imag[:, 0:1]
        nyquist_row = jnp.where(on_first, packed, 0.0)
        got_imag = jnp.concatenate(
            [jnp.where(on_first, 0.0, packed), got_imag[:, 1:], jnp.zeros_like(packed)], axis=1
        )
        got_real = jnp.concatenate([got_real, nyquist_row], axis=1)
        got_real, got_imag = rotate(got_real, got_imag, big_cos, -big_sin)
        spectra.append(row_forward(got_real, got_imag, -1.0))

    head_real, head_imag = complex_product(*spectra[0], *spectra[2])
    rest_real, rest_imag = complex_product(*spectra[1], *spectra[3])
    back_real, back_imag = row_inverse(head_real + rest_real, head_imag + rest_imag, 1.0)
    back_real, back_imag = rotate(back_real, back_imag, big_cos, big_sin)
    first_imag = jnp.where(on_first, back_real[:, rows_here:], back_imag[:, 0:1])
    back_imag = jnp.concatenate([first_imag, back_imag[:, 1:rows_here]], axis=1)
    back_real = back_real[:, :rows_here]
    payload = jnp.stack([back_real, back_imag], axis=1)
    got = lax.all_to_all(payload, "fft", 0, 0, tiled=True)
    full_real = got[:, 0].reshape(row_count, local_cols)
    full_imag = got[:, 1].reshape(row_count, local_cols)
    nyquist = full_imag[0]
    full_real = full_real.at[0].multiply(0.5)
    full_imag = full_imag.at[0].set(0.0)
    values = column_transform(full_real, full_imag, 2 * row_count, 1.0)
    alternating = (1 - 2 * (iota(2 * row_count) % 2)).astype(jnp.float32)
    values = 2.0 * values + alternating[:, None] * nyquist[None, :]
    out_scale = 1.0 / (length * math.sqrt(length // 2))
    return (values * out_scale)[None]


def solution(mesh):
    placed = (
        P("entry", "fft"),
        P("entry", "fft"),
        P("entry", "fft"),
        P("entry", "fft"),
        P("entry", "fft"),
        P("entry", "fft"),
        P("entry", "fft"),
        P("entry", "fft"),
    )
    return jax.shard_map(
        local, mesh=mesh, in_specs=placed, out_specs=P("entry", None, "fft"), check_vma=False
    )
```

```python
import math

import jax
import jax.numpy as jnp
from jax import lax
from jax.sharding import PartitionSpec as P

RADIX = 64


exact_precision = lax.Precision.HIGHEST


def contract(pattern, left_op, right_op):
    return jnp.einsum(
        pattern, left_op, right_op, precision=exact_precision, preferred_element_type=jnp.float32
    )


def iota(count):
    return jnp.arange(count, dtype=jnp.int32)


def angle_table(first_part, second_part, length, sense_sign):
    turns = first_part[:, None] * second_part[None, :] % length
    phase_angle = turns.astype(jnp.float32) * (2.0 * math.pi / length)
    return (jnp.cos(phase_angle), sense_sign * jnp.sin(phase_angle))


def rotate(real_part, imag_part, cosine, sine):
    return (real_part * cosine - imag_part * sine, real_part * sine + imag_part * cosine)


def complex_product(left_real, left_imag, right_real, right_imag):
    return (
        left_real * right_real - left_imag * right_imag,
        left_real * right_imag + left_imag * right_real,
    )


def table_left(pattern, table, real_part, imag_part):
    cosine, sine = table
    if imag_part is None:
        return contract(pattern, cosine, real_part), contract(pattern, sine, real_part)
    return (
        contract(pattern, cosine, real_part) - contract(pattern, sine, imag_part),
        contract(pattern, sine, real_part) + contract(pattern, cosine, imag_part),
    )


def table_right(pattern, real_part, imag_part, table):
    cosine, sine = table
    return (
        contract(pattern, real_part, cosine) - contract(pattern, imag_part, sine),
        contract(pattern, real_part, sine) + contract(pattern, imag_part, cosine),
    )


def digits(limbs):
    return (limbs.astype(jnp.float32) - 32768.0) * (1.0 / 32768.0)


def column_half(values):
    row_count, column_count = values.shape
    length = 2 * row_count
    inner_size = length // RADIX
    outer_count = row_count // inner_size
    first = angle_table(iota(RADIX), iota(outer_count), RADIX, -1.0)
    flat = values.reshape(outer_count, inner_size * column_count)
    step_real, step_imag = table_left("ja,an->jn", first, flat, None)
    step_real = step_real.reshape(RADIX, inner_size, column_count)
    step_imag = step_imag.reshape(RADIX, inner_size, column_count)
    twist_cos, twist_sin = angle_table(iota(RADIX), iota(inner_size), length, -1.0)
    step_real, step_imag = lax.optimization_barrier(rotate(
        step_real, step_imag, twist_cos[:, :, None], twist_sin[:, :, None]
    ))
    second = angle_table(iota(inner_size // 2), iota(inner_size), inner_size, -1.0)
    final_real, final_imag = table_left("mb,jbc->mjc", second, step_real, step_imag)
    alternating = (1 - 2 * (iota(inner_size) % 2)).astype(jnp.float32)
    nyquist = contract("b,bc->c", alternating, step_real[0])
    final_imag = final_imag.at[0, 0].set(nyquist)
    return final_real, final_imag


def column_transform(real_part, imag_part, length, sense_sign):
    inner_size = length // RADIX
    outer_count = real_part.shape[0] // inner_size
    column_count = real_part.shape[1]
    first = angle_table(iota(RADIX), iota(outer_count), RADIX, sense_sign)
    flat_real = real_part.reshape(outer_count, inner_size * column_count)
    flat_imag = imag_part.reshape(outer_count, inner_size * column_count)
    step_real, step_imag = table_left("ja,an->jn", first, flat_real, flat_imag)
    step_real = step_real.reshape(RADIX, inner_size, column_count)
    step_imag = step_imag.reshape(RADIX, inner_size, column_count)
    twist_cos, twist_sin = angle_table(iota(RADIX), iota(inner_size), length, sense_sign)
    step_real, step_imag = rotate(
        step_real, step_imag, twist_cos[:, :, None], twist_sin[:, :, None]
    )
    second_cos, second_sin = angle_table(iota(inner_size), iota(inner_size), inner_size, sense_sign)
    final_real = contract("mb,kbc->mkc", second_cos, step_real) - contract(
        "mb,kbc->mkc", second_sin, step_imag
    )
    return final_real.reshape(length, column_count)


def row_forward(real_part, imag_part, sense_sign):
    source_count, _, column_count = real_part.shape
    length = source_count * column_count
    first = angle_table(iota(source_count), iota(source_count), source_count, sense_sign)
    step_real, step_imag = table_left("us,src->urc", first, real_part, imag_part)
    twist_cos, twist_sin = angle_table(iota(source_count), iota(column_count), length, sense_sign)
    step_real, step_imag = rotate(
        step_real, step_imag, twist_cos[:, None, :], twist_sin[:, None, :]
    )
    second = angle_table(iota(column_count), iota(column_count), column_count, sense_sign)
    return table_right("urc,cv->urv", step_real, step_imag, second)


def row_inverse(real_part, imag_part, sense_sign):
    source_count, _, column_count = real_part.shape
    length = source_count * column_count
    second = angle_table(iota(column_count), iota(column_count), column_count, sense_sign)
    step_real, step_imag = table_right("urv,vc->urc", real_part, imag_part, second)
    twist_cos, twist_sin = angle_table(iota(source_count), iota(column_count), length, sense_sign)
    step_real, step_imag = rotate(
        step_real, step_imag, twist_cos[:, None, :], twist_sin[:, None, :]
    )
    first = angle_table(iota(source_count), iota(source_count), source_count, sense_sign)
    return table_left("su,urc->src", first, step_real, step_imag)


def local(
    left_zero_zero,
    left_zero_one,
    left_one_zero,
    left_one_one,
    right_zero_zero,
    right_zero_one,
    right_one_zero,
    right_one_one,
):
    lefts = [[left_zero_zero, left_zero_one], [left_one_zero, left_one_one]]
    rights = [[right_zero_zero, right_zero_one], [right_one_zero, right_one_one]]
    entry_count = lax.axis_size("entry")
    fft_count = lax.axis_size("fft")
    fft_place = lax.axis_index("fft")
    on_first = fft_place == 0
    local_cols = left_zero_zero.shape[1]
    row_count = left_zero_zero.shape[0] * entry_count
    length = 2 * row_count * local_cols * fft_count
    column_count = local_cols * fft_count
    rows_here = 2 * row_count // (2 * fft_count)

    held_k1 = jnp.concatenate(
        [fft_place * rows_here + iota(rows_here), jnp.full((1,), row_count, jnp.int32)]
    )
    source_cols = (iota(fft_count)[:, None] * local_cols + iota(local_cols)[None, :])
    turns = source_cols[:, None, :] * held_k1[None, :, None] % length
    big_angle = turns.astype(jnp.float32) * (2.0 * math.pi / length)
    big_cos = jnp.cos(big_angle)
    big_sin = jnp.sin(big_angle)

    spectra = []
    for member in range(4):
        if member < 2:
            pieces = [lefts[target // 2][member] for target in range(4)]
        else:
            pieces = [rights[member - 2][target % 2] for target in range(4)]
        outgoing = digits(jnp.stack(pieces))
        arrived = lax.all_to_all(outgoing, "entry", 0, 0, tiled=True)
        arrived = arrived.reshape(row_count, local_cols)
        half_real, half_imag = column_half(arrived)
        payload = jnp.stack([half_real, half_imag], axis=1)
        got = lax.all_to_all(payload, "fft", 0, 0, tiled=True)
        got_real = got[:, 0]
        got_imag = got[:, 1]
        packed = got_imag[:, 0:1]
        nyquist_row = jnp.where(on_first, packed, 0.0)
        got_imag = jnp.concatenate(
            [jnp.where(on_first, 0.0, packed), got_imag[:, 1:], jnp.zeros_like(packed)], axis=1
        )
        got_real = jnp.concatenate([got_real, nyquist_row], axis=1)
        got_real, got_imag = lax.optimization_barrier(
            rotate(got_real, got_imag, big_cos, -big_sin)
        )
        spectra.append(row_forward(got_real, got_imag, -1.0))

    head_real, head_imag = complex_product(*spectra[0], *spectra[2])
    rest_real, rest_imag = complex_product(*spectra[1], *spectra[3])
    back_real, back_imag = row_inverse(head_real + rest_real, head_imag + rest_imag, 1.0)
    back_real, back_imag = rotate(back_real, back_imag, big_cos, big_sin)
    first_imag = jnp.where(on_first, back_real[:, rows_here:], back_imag[:, 0:1])
    back_imag = jnp.concatenate([first_imag, back_imag[:, 1:rows_here]], axis=1)
    back_real = back_real[:, :rows_here]
    payload = jnp.stack([back_real, back_imag], axis=1)
    got = lax.all_to_all(payload, "fft", 0, 0, tiled=True)
    full_real = got[:, 0].reshape(row_count, local_cols)
    full_imag = got[:, 1].reshape(row_count, local_cols)
    nyquist = full_imag[0]
    full_real = full_real.at[0].multiply(0.5)
    full_imag = full_imag.at[0].set(0.0)
    values = column_transform(full_real, full_imag, 2 * row_count, 1.0)
    alternating = (1 - 2 * (iota(2 * row_count) % 2)).astype(jnp.float32)
    values = 2.0 * values + alternating[:, None] * nyquist[None, :]
    out_scale = 1.0 / (length * math.sqrt(length // 2))
    return (values * out_scale)[None]


def solution(mesh):
    placed = (
        P("entry", "fft"),
        P("entry", "fft"),
        P("entry", "fft"),
        P("entry", "fft"),
        P("entry", "fft"),
        P("entry", "fft"),
        P("entry", "fft"),
        P("entry", "fft"),
    )
    return jax.shard_map(
        local, mesh=mesh, in_specs=placed, out_specs=P("entry", None, "fft"), check_vma=False
    )
```

```python
import math

import jax
import jax.numpy as jnp
from jax import lax
from jax.sharding import PartitionSpec as P

RADIX = 64


exact_precision = lax.Precision.HIGHEST


def contract(pattern, left_op, right_op):
    return jnp.einsum(
        pattern, left_op, right_op, precision=exact_precision, preferred_element_type=jnp.float32
    )


def iota(count):
    return jnp.arange(count, dtype=jnp.int32)


def angle_table(first_part, second_part, length, sense_sign):
    turns = first_part[:, None] * second_part[None, :] % length
    phase_angle = turns.astype(jnp.float32) * (2.0 * math.pi / length)
    return lax.optimization_barrier((jnp.cos(phase_angle), sense_sign * jnp.sin(phase_angle)))


def rotate(real_part, imag_part, cosine, sine):
    return (real_part * cosine - imag_part * sine, real_part * sine + imag_part * cosine)


def complex_product(left_real, left_imag, right_real, right_imag):
    return (
        left_real * right_real - left_imag * right_imag,
        left_real * right_imag + left_imag * right_real,
    )


def table_left(pattern, table, real_part, imag_part):
    cosine, sine = table
    if imag_part is None:
        return contract(pattern, cosine, real_part), contract(pattern, sine, real_part)
    return (
        contract(pattern, cosine, real_part) - contract(pattern, sine, imag_part),
        contract(pattern, sine, real_part) + contract(pattern, cosine, imag_part),
    )


def table_right(pattern, real_part, imag_part, table):
    cosine, sine = table
    return (
        contract(pattern, real_part, cosine) - contract(pattern, imag_part, sine),
        contract(pattern, real_part, sine) + contract(pattern, imag_part, cosine),
    )


def digits(limbs):
    return (limbs.astype(jnp.float32) - 32768.0) * (1.0 / 32768.0)


def column_half(values):
    row_count, column_count = values.shape
    length = 2 * row_count
    inner_size = length // RADIX
    outer_count = row_count // inner_size
    first = angle_table(iota(RADIX), iota(outer_count), RADIX, -1.0)
    flat = values.reshape(outer_count, inner_size * column_count)
    step_real, step_imag = table_left("ja,an->jn", first, flat, None)
    step_real = step_real.reshape(RADIX, inner_size, column_count)
    step_imag = step_imag.reshape(RADIX, inner_size, column_count)
    twist_cos, twist_sin = angle_table(iota(RADIX), iota(inner_size), length, -1.0)
    step_real, step_imag = lax.optimization_barrier(rotate(
        step_real, step_imag, twist_cos[:, :, None], twist_sin[:, :, None]
    ))
    second = angle_table(iota(inner_size // 2), iota(inner_size), inner_size, -1.0)
    final_real, final_imag = table_left("mb,jbc->mjc", second, step_real, step_imag)
    alternating = (1 - 2 * (iota(inner_size) % 2)).astype(jnp.float32)
    nyquist = contract("b,bc->c", alternating, step_real[0])
    final_imag = final_imag.at[0, 0].set(nyquist)
    return final_real, final_imag


def column_part(real_part, imag_part, length, sense_sign, offset):
    outer_count, part_size, column_count = real_part.shape
    inner_size = length // RADIX
    first = angle_table(iota(RADIX), iota(outer_count), RADIX, sense_sign)
    flat_real = real_part.reshape(outer_count, part_size * column_count)
    flat_imag = imag_part.reshape(outer_count, part_size * column_count)
    step_real, step_imag = table_left("ja,an->jn", first, flat_real, flat_imag)
    step_real = step_real.reshape(RADIX, part_size, column_count)
    step_imag = step_imag.reshape(RADIX, part_size, column_count)
    twist_cos, twist_sin = angle_table(iota(RADIX), offset + iota(part_size), length, sense_sign)
    step_real, step_imag = lax.optimization_barrier(rotate(
        step_real, step_imag, twist_cos[:, :, None], twist_sin[:, :, None]
    ))
    second_cos, second_sin = angle_table(iota(inner_size), offset + iota(part_size), inner_size, sense_sign)
    final_real = contract("mb,kbc->mkc", second_cos, step_real) - contract(
        "mb,kbc->mkc", second_sin, step_imag
    )
    return final_real.reshape(length, column_count)


def row_forward(real_part, imag_part, sense_sign):
    source_count, _, column_count = real_part.shape
    length = source_count * column_count
    first = angle_table(iota(source_count), iota(source_count), source_count, sense_sign)
    step_real, step_imag = table_left("us,src->urc", first, real_part, imag_part)
    twist_cos, twist_sin = angle_table(iota(source_count), iota(column_count), length, sense_sign)
    step_real, step_imag = rotate(
        step_real, step_imag, twist_cos[:, None, :], twist_sin[:, None, :]
    )
    second = angle_table(iota(column_count), iota(column_count), column_count, sense_sign)
    return table_right("urc,cv->urv", step_real, step_imag, second)


def row_inverse(real_part, imag_part, sense_sign):
    source_count, _, column_count = real_part.shape
    length = source_count * column_count
    second = angle_table(iota(column_count), iota(column_count), column_count, sense_sign)
    step_real, step_imag = table_right("urv,vc->urc", real_part, imag_part, second)
    twist_cos, twist_sin = angle_table(iota(source_count), iota(column_count), length, sense_sign)
    step_real, step_imag = rotate(
        step_real, step_imag, twist_cos[:, None, :], twist_sin[:, None, :]
    )
    first = angle_table(iota(source_count), iota(source_count), source_count, sense_sign)
    return table_left("su,urc->src", first, step_real, step_imag)


def local(
    left_zero_zero,
    left_zero_one,
    left_one_zero,
    left_one_one,
    right_zero_zero,
    right_zero_one,
    right_one_zero,
    right_one_one,
):
    lefts = [[left_zero_zero, left_zero_one], [left_one_zero, left_one_one]]
    rights = [[right_zero_zero, right_zero_one], [right_one_zero, right_one_one]]
    entry_count = lax.axis_size("entry")
    fft_count = lax.axis_size("fft")
    fft_place = lax.axis_index("fft")
    on_first = fft_place == 0
    local_cols = left_zero_zero.shape[1]
    row_count = left_zero_zero.shape[0] * entry_count
    length = 2 * row_count * local_cols * fft_count
    column_count = local_cols * fft_count
    rows_here = 2 * row_count // (2 * fft_count)

    held_k1 = jnp.concatenate(
        [fft_place * rows_here + iota(rows_here), jnp.full((1,), row_count, jnp.int32)]
    )
    source_cols = (iota(fft_count)[:, None] * local_cols + iota(local_cols)[None, :])
    turns = source_cols[:, None, :] * held_k1[None, :, None] % length
    big_angle = turns.astype(jnp.float32) * (2.0 * math.pi / length)
    big_cos, big_sin = lax.optimization_barrier((jnp.cos(big_angle), jnp.sin(big_angle)))

    spectra = []
    for member in range(4):
        if member < 2:
            pieces = [lefts[target // 2][member] for target in range(4)]
        else:
            pieces = [rights[member - 2][target % 2] for target in range(4)]
        outgoing = digits(jnp.stack(pieces))
        arrived = lax.all_to_all(outgoing, "entry", 0, 0, tiled=True)
        arrived = arrived.reshape(row_count, local_cols)
        half_real, half_imag = column_half(arrived)
        payload = jnp.stack([half_real, half_imag], axis=1)
        got = lax.all_to_all(payload, "fft", 0, 0, tiled=True)
        got_real = got[:, 0]
        got_imag = got[:, 1]
        packed = got_imag[:, 0:1]
        nyquist_row = jnp.where(on_first, packed, 0.0)
        got_imag = jnp.concatenate(
            [jnp.where(on_first, 0.0, packed), got_imag[:, 1:], jnp.zeros_like(packed)], axis=1
        )
        got_real = jnp.concatenate([got_real, nyquist_row], axis=1)
        got_real, got_imag = lax.optimization_barrier(
            rotate(got_real, got_imag, big_cos, -big_sin)
        )
        spectra.append(row_forward(got_real, got_imag, -1.0))

    head_real, head_imag = complex_product(*spectra[0], *spectra[2])
    rest_real, rest_imag = complex_product(*spectra[1], *spectra[3])
    mixed_real = head_real + rest_real
    mixed_imag = head_imag + rest_imag
    part_rows = rows_here // 2
    pieces = (
        (slice(0, part_rows), True),
        (slice(part_rows, rows_here), False),
    )
    values = None
    nyquist = None
    for rows, with_nyquist in pieces:
        part_real = mixed_real[:, rows]
        part_imag = mixed_imag[:, rows]
        part_cos = big_cos[:, rows]
        part_sin = big_sin[:, rows]
        if with_nyquist:
            part_real = jnp.concatenate([part_real, mixed_real[:, rows_here:]], axis=1)
            part_imag = jnp.concatenate([part_imag, mixed_imag[:, rows_here:]], axis=1)
            part_cos = jnp.concatenate([part_cos, big_cos[:, rows_here:]], axis=1)
            part_sin = jnp.concatenate([part_sin, big_sin[:, rows_here:]], axis=1)
        back_real, back_imag = row_inverse(part_real, part_imag, 1.0)
        back_real, back_imag = rotate(back_real, back_imag, part_cos, part_sin)
        if with_nyquist:
            first_imag = jnp.where(on_first, back_real[:, part_rows:], back_imag[:, 0:1])
            back_imag = jnp.concatenate([first_imag, back_imag[:, 1:part_rows]], axis=1)
            back_real = back_real[:, :part_rows]
        payload = jnp.stack([back_real, back_imag], axis=1)
        got = lax.all_to_all(payload, "fft", 0, 0, tiled=True)
        full_real = got[:, 0]
        full_imag = got[:, 1]
        if with_nyquist:
            nyquist = full_imag[0, 0]
            full_real = full_real.at[0, 0].multiply(0.5)
            full_imag = full_imag.at[0, 0].set(0.0)
        part = column_part(full_real, full_imag, 2 * row_count, 1.0, rows.start)
        values = part if values is None else values + part
    alternating = (1 - 2 * (iota(2 * row_count) % 2)).astype(jnp.float32)
    values = 2.0 * values + alternating[:, None] * nyquist[None, :]
    out_scale = 1.0 / (length * math.sqrt(length // 2))
    return (values * out_scale)[None]


def solution(mesh):
    placed = (
        P("entry", "fft"),
        P("entry", "fft"),
        P("entry", "fft"),
        P("entry", "fft"),
        P("entry", "fft"),
        P("entry", "fft"),
        P("entry", "fft"),
        P("entry", "fft"),
    )
    return jax.shard_map(
        local, mesh=mesh, in_specs=placed, out_specs=P("entry", None, "fft"), check_vma=False
    )
```

```python
import math

import jax
import jax.numpy as jnp
from jax import lax
from jax.sharding import PartitionSpec as P

RADIX = 64


exact_precision = lax.Precision.HIGHEST


def contract(pattern, left_op, right_op):
    return jnp.einsum(
        pattern, left_op, right_op, precision=exact_precision, preferred_element_type=jnp.float32
    )


def iota(count):
    return jnp.arange(count, dtype=jnp.int32)


def angle_table(first_part, second_part, length, sense_sign):
    turns = first_part[:, None] * second_part[None, :] % length
    phase_angle = turns.astype(jnp.float32) * (2.0 * math.pi / length)
    return lax.optimization_barrier((jnp.cos(phase_angle), sense_sign * jnp.sin(phase_angle)))


def rotate(real_part, imag_part, cosine, sine):
    return (real_part * cosine - imag_part * sine, real_part * sine + imag_part * cosine)


def complex_product(left_real, left_imag, right_real, right_imag):
    return (
        left_real * right_real - left_imag * right_imag,
        left_real * right_imag + left_imag * right_real,
    )


def table_left(pattern, table, real_part, imag_part):
    cosine, sine = table
    if imag_part is None:
        return contract(pattern, cosine, real_part), contract(pattern, sine, real_part)
    return (
        contract(pattern, cosine, real_part) - contract(pattern, sine, imag_part),
        contract(pattern, sine, real_part) + contract(pattern, cosine, imag_part),
    )


def table_right(pattern, real_part, imag_part, table):
    cosine, sine = table
    return (
        contract(pattern, real_part, cosine) - contract(pattern, imag_part, sine),
        contract(pattern, real_part, sine) + contract(pattern, imag_part, cosine),
    )


def digits(limbs):
    return (limbs.astype(jnp.float32) - 32768.0) * (1.0 / 32768.0)


def column_half(values):
    row_count, column_count = values.shape
    length = 2 * row_count
    inner_size = length // RADIX
    outer_count = row_count // inner_size
    first = angle_table(iota(RADIX), iota(outer_count), RADIX, -1.0)
    flat = values.reshape(outer_count, inner_size * column_count)
    step_real, step_imag = table_left("ja,an->jn", first, flat, None)
    step_real = step_real.reshape(RADIX, inner_size, column_count)
    step_imag = step_imag.reshape(RADIX, inner_size, column_count)
    twist_cos, twist_sin = angle_table(iota(RADIX), iota(inner_size), length, -1.0)
    step_real, step_imag = lax.optimization_barrier(rotate(
        step_real, step_imag, twist_cos[:, :, None], twist_sin[:, :, None]
    ))
    second = angle_table(iota(inner_size // 2), iota(inner_size), inner_size, -1.0)
    final_real, final_imag = table_left("mb,jbc->mjc", second, step_real, step_imag)
    alternating = (1 - 2 * (iota(inner_size) % 2)).astype(jnp.float32)
    nyquist = contract("b,bc->c", alternating, step_real[0])
    final_imag = final_imag.at[0, 0].set(nyquist)
    return final_real, final_imag


def column_part(real_part, imag_part, length, sense_sign, offset):
    outer_count, part_size, column_count = real_part.shape
    inner_size = length // RADIX
    first = angle_table(iota(RADIX), iota(outer_count), RADIX, sense_sign)
    flat_real = real_part.reshape(outer_count, part_size * column_count)
    flat_imag = imag_part.reshape(outer_count, part_size * column_count)
    step_real, step_imag = table_left("ja,an->jn", first, flat_real, flat_imag)
    step_real = step_real.reshape(RADIX, part_size, column_count)
    step_imag = step_imag.reshape(RADIX, part_size, column_count)
    twist_cos, twist_sin = angle_table(iota(RADIX), offset + iota(part_size), length, sense_sign)
    step_real, step_imag = lax.optimization_barrier(rotate(
        step_real, step_imag, twist_cos[:, :, None], twist_sin[:, :, None]
    ))
    second_cos, second_sin = angle_table(iota(inner_size), offset + iota(part_size), inner_size, sense_sign)
    final_real = contract("mb,kbc->mkc", second_cos, step_real) - contract(
        "mb,kbc->mkc", second_sin, step_imag
    )
    return final_real.reshape(length, column_count)


def row_forward(real_part, imag_part, sense_sign):
    source_count, _, column_count = real_part.shape
    length = source_count * column_count
    first = angle_table(iota(source_count), iota(source_count), source_count, sense_sign)
    step_real, step_imag = table_left("us,src->urc", first, real_part, imag_part)
    twist_cos, twist_sin = angle_table(iota(source_count), iota(column_count), length, sense_sign)
    step_real, step_imag = rotate(
        step_real, step_imag, twist_cos[:, None, :], twist_sin[:, None, :]
    )
    second = angle_table(iota(column_count), iota(column_count), column_count, sense_sign)
    return table_right("urc,cv->urv", step_real, step_imag, second)


def row_inverse(real_part, imag_part, sense_sign):
    source_count, _, column_count = real_part.shape
    length = source_count * column_count
    second = angle_table(iota(column_count), iota(column_count), column_count, sense_sign)
    step_real, step_imag = table_right("urv,vc->urc", real_part, imag_part, second)
    twist_cos, twist_sin = angle_table(iota(source_count), iota(column_count), length, sense_sign)
    step_real, step_imag = rotate(
        step_real, step_imag, twist_cos[:, None, :], twist_sin[:, None, :]
    )
    first = angle_table(iota(source_count), iota(source_count), source_count, sense_sign)
    return table_left("su,urc->src", first, step_real, step_imag)


def local(
    left_zero_zero,
    left_zero_one,
    left_one_zero,
    left_one_one,
    right_zero_zero,
    right_zero_one,
    right_one_zero,
    right_one_one,
):
    lefts = [[left_zero_zero, left_zero_one], [left_one_zero, left_one_one]]
    rights = [[right_zero_zero, right_zero_one], [right_one_zero, right_one_one]]
    entry_count = lax.axis_size("entry")
    fft_count = lax.axis_size("fft")
    fft_place = lax.axis_index("fft")
    on_first = fft_place == 0
    local_cols = left_zero_zero.shape[1]
    row_count = left_zero_zero.shape[0] * entry_count
    length = 2 * row_count * local_cols * fft_count
    column_count = local_cols * fft_count
    rows_here = 2 * row_count // (2 * fft_count)

    held_k1 = jnp.concatenate(
        [fft_place * rows_here + iota(rows_here), jnp.full((1,), row_count, jnp.int32)]
    )
    source_cols = (iota(fft_count)[:, None] * local_cols + iota(local_cols)[None, :])
    turns = source_cols[:, None, :] * held_k1[None, :, None] % length
    big_angle = turns.astype(jnp.float32) * (2.0 * math.pi / length)
    big_cos, big_sin = lax.optimization_barrier((jnp.cos(big_angle), jnp.sin(big_angle)))

    member_pieces = (
        [lefts[target // 2][target % 2] for target in range(entry_count)],
        [rights[target % 2][target % 2] for target in range(entry_count)],
        [rights[1 - target % 2][target % 2] for target in range(entry_count)],
    )
    spectra = []
    for pieces in member_pieces:
        outgoing = digits(jnp.stack(pieces))
        arrived = lax.all_to_all(outgoing, "entry", 0, 0, tiled=True)
        arrived = arrived.reshape(row_count, local_cols)
        half_real, half_imag = column_half(arrived)
        payload = jnp.stack([half_real, half_imag], axis=1)
        got = lax.all_to_all(payload, "fft", 0, 0, tiled=True)
        got_real = got[:, 0]
        got_imag = got[:, 1]
        packed = got_imag[:, 0:1]
        nyquist_row = jnp.where(on_first, packed, 0.0)
        got_imag = jnp.concatenate(
            [jnp.where(on_first, 0.0, packed), got_imag[:, 1:], jnp.zeros_like(packed)], axis=1
        )
        got_real = jnp.concatenate([got_real, nyquist_row], axis=1)
        got_real, got_imag = lax.optimization_barrier(
            rotate(got_real, got_imag, big_cos, -big_sin)
        )
        spectra.append(row_forward(got_real, got_imag, -1.0))

    sibling_pairs = [(place, place ^ 1) for place in range(entry_count)]
    sibling = lax.ppermute(jnp.stack(spectra[0]), "entry", sibling_pairs)
    head_real, head_imag = complex_product(*spectra[0], *spectra[1])
    rest_real, rest_imag = complex_product(sibling[0], sibling[1], *spectra[2])
    mixed_real = head_real + rest_real
    mixed_imag = head_imag + rest_imag
    part_rows = rows_here // 2
    pieces = (
        (slice(0, part_rows), True),
        (slice(part_rows, rows_here), False),
    )
    values = None
    nyquist = None
    for rows, with_nyquist in pieces:
        part_real = mixed_real[:, rows]
        part_imag = mixed_imag[:, rows]
        part_cos = big_cos[:, rows]
        part_sin = big_sin[:, rows]
        if with_nyquist:
            part_real = jnp.concatenate([part_real, mixed_real[:, rows_here:]], axis=1)
            part_imag = jnp.concatenate([part_imag, mixed_imag[:, rows_here:]], axis=1)
            part_cos = jnp.concatenate([part_cos, big_cos[:, rows_here:]], axis=1)
            part_sin = jnp.concatenate([part_sin, big_sin[:, rows_here:]], axis=1)
        back_real, back_imag = row_inverse(part_real, part_imag, 1.0)
        back_real, back_imag = rotate(back_real, back_imag, part_cos, part_sin)
        if with_nyquist:
            first_imag = jnp.where(on_first, back_real[:, part_rows:], back_imag[:, 0:1])
            back_imag = jnp.concatenate([first_imag, back_imag[:, 1:part_rows]], axis=1)
            back_real = back_real[:, :part_rows]
        payload = jnp.stack([back_real, back_imag], axis=1)
        got = lax.all_to_all(payload, "fft", 0, 0, tiled=True)
        full_real = got[:, 0]
        full_imag = got[:, 1]
        if with_nyquist:
            nyquist = full_imag[0, 0]
            full_real = full_real.at[0, 0].multiply(0.5)
            full_imag = full_imag.at[0, 0].set(0.0)
        part = column_part(full_real, full_imag, 2 * row_count, 1.0, rows.start)
        values = part if values is None else values + part
    alternating = (1 - 2 * (iota(2 * row_count) % 2)).astype(jnp.float32)
    values = 2.0 * values + alternating[:, None] * nyquist[None, :]
    out_scale = 1.0 / (length * math.sqrt(length // 2))
    return (values * out_scale)[None]


def solution(mesh):
    placed = (
        P("entry", "fft"),
        P("entry", "fft"),
        P("entry", "fft"),
        P("entry", "fft"),
        P("entry", "fft"),
        P("entry", "fft"),
        P("entry", "fft"),
        P("entry", "fft"),
    )
    return jax.shard_map(
        local, mesh=mesh, in_specs=placed, out_specs=P("entry", None, "fft"), check_vma=False
    )
```

```python
import math

import jax
import jax.numpy as jnp
from jax import lax
from jax.sharding import PartitionSpec as P

RADIX = 64


exact_precision = lax.Precision.HIGHEST


def contract(pattern, left_op, right_op):
    return jnp.einsum(
        pattern, left_op, right_op, precision=exact_precision, preferred_element_type=jnp.float32
    )


def iota(count):
    return jnp.arange(count, dtype=jnp.int32)


def angle_table(first_part, second_part, length, sense_sign):
    turns = first_part[:, None] * second_part[None, :] % length
    phase_angle = turns.astype(jnp.float32) * (2.0 * math.pi / length)
    return lax.optimization_barrier((jnp.cos(phase_angle), sense_sign * jnp.sin(phase_angle)))


def rotate(real_part, imag_part, cosine, sine):
    return (real_part * cosine - imag_part * sine, real_part * sine + imag_part * cosine)


def complex_product(left_real, left_imag, right_real, right_imag):
    return (
        left_real * right_real - left_imag * right_imag,
        left_real * right_imag + left_imag * right_real,
    )


def table_left(pattern, table, real_part, imag_part):
    cosine, sine = table
    if imag_part is None:
        return contract(pattern, cosine, real_part), contract(pattern, sine, real_part)
    return (
        contract(pattern, cosine, real_part) - contract(pattern, sine, imag_part),
        contract(pattern, sine, real_part) + contract(pattern, cosine, imag_part),
    )


def table_right(pattern, real_part, imag_part, table):
    cosine, sine = table
    return (
        contract(pattern, real_part, cosine) - contract(pattern, imag_part, sine),
        contract(pattern, real_part, sine) + contract(pattern, imag_part, cosine),
    )


def digits(limbs):
    return (limbs.astype(jnp.float32) - 32768.0) * (1.0 / 32768.0)


def column_half(values, outer_index):
    row_count, column_count = values.shape
    length = 2 * row_count
    inner_size = length // RADIX
    outer_count = row_count // inner_size
    first = angle_table(iota(RADIX), outer_index, RADIX, -1.0)
    flat = values.reshape(outer_count, inner_size * column_count)
    step_real, step_imag = table_left("ja,an->jn", first, flat, None)
    step_real = step_real.reshape(RADIX, inner_size, column_count)
    step_imag = step_imag.reshape(RADIX, inner_size, column_count)
    twist_cos, twist_sin = angle_table(iota(RADIX), iota(inner_size), length, -1.0)
    step_real, step_imag = lax.optimization_barrier(rotate(
        step_real, step_imag, twist_cos[:, :, None], twist_sin[:, :, None]
    ))
    second = angle_table(iota(inner_size // 2), iota(inner_size), inner_size, -1.0)
    final_real, final_imag = table_left("mb,jbc->mjc", second, step_real, step_imag)
    alternating = (1 - 2 * (iota(inner_size) % 2)).astype(jnp.float32)
    nyquist = contract("b,bc->c", alternating, step_real[0])
    final_imag = final_imag.at[0, 0].set(nyquist)
    return final_real, final_imag


def column_part(real_part, imag_part, length, sense_sign, offset):
    outer_count, part_size, column_count = real_part.shape
    inner_size = length // RADIX
    first = angle_table(iota(RADIX), iota(outer_count), RADIX, sense_sign)
    flat_real = real_part.reshape(outer_count, part_size * column_count)
    flat_imag = imag_part.reshape(outer_count, part_size * column_count)
    step_real, step_imag = table_left("ja,an->jn", first, flat_real, flat_imag)
    step_real = step_real.reshape(RADIX, part_size, column_count)
    step_imag = step_imag.reshape(RADIX, part_size, column_count)
    twist_cos, twist_sin = angle_table(iota(RADIX), offset + iota(part_size), length, sense_sign)
    step_real, step_imag = lax.optimization_barrier(rotate(
        step_real, step_imag, twist_cos[:, :, None], twist_sin[:, :, None]
    ))
    second_cos, second_sin = angle_table(iota(inner_size), offset + iota(part_size), inner_size, sense_sign)
    final_real = contract("mb,kbc->mkc", second_cos, step_real) - contract(
        "mb,kbc->mkc", second_sin, step_imag
    )
    return final_real.reshape(length, column_count)


def row_forward(real_part, imag_part, sense_sign):
    source_count, _, column_count = real_part.shape
    length = source_count * column_count
    first = angle_table(iota(source_count), iota(source_count), source_count, sense_sign)
    step_real, step_imag = table_left("us,src->urc", first, real_part, imag_part)
    twist_cos, twist_sin = angle_table(iota(source_count), iota(column_count), length, sense_sign)
    step_real, step_imag = rotate(
        step_real, step_imag, twist_cos[:, None, :], twist_sin[:, None, :]
    )
    second = angle_table(iota(column_count), iota(column_count), column_count, sense_sign)
    return table_right("urc,cv->urv", step_real, step_imag, second)


def row_inverse(real_part, imag_part, sense_sign):
    source_count, _, column_count = real_part.shape
    length = source_count * column_count
    second = angle_table(iota(column_count), iota(column_count), column_count, sense_sign)
    step_real, step_imag = table_right("urv,vc->urc", real_part, imag_part, second)
    twist_cos, twist_sin = angle_table(iota(source_count), iota(column_count), length, sense_sign)
    step_real, step_imag = rotate(
        step_real, step_imag, twist_cos[:, None, :], twist_sin[:, None, :]
    )
    first = angle_table(iota(source_count), iota(source_count), source_count, sense_sign)
    return table_left("su,urc->src", first, step_real, step_imag)


def local(
    left_zero_zero,
    left_zero_one,
    left_one_zero,
    left_one_one,
    right_zero_zero,
    right_zero_one,
    right_one_zero,
    right_one_one,
):
    lefts = [[left_zero_zero, left_zero_one], [left_one_zero, left_one_one]]
    rights = [[right_zero_zero, right_zero_one], [right_one_zero, right_one_one]]
    entry_count = lax.axis_size("entry")
    fft_count = lax.axis_size("fft")
    fft_place = lax.axis_index("fft")
    on_first = fft_place == 0
    local_cols = left_zero_zero.shape[1]
    row_count = left_zero_zero.shape[0] * entry_count
    length = 2 * row_count * local_cols * fft_count
    column_count = local_cols * fft_count
    rows_here = 2 * row_count // (2 * fft_count)

    held_k1 = jnp.concatenate(
        [fft_place * rows_here + iota(rows_here), jnp.full((1,), row_count, jnp.int32)]
    )
    source_cols = (iota(fft_count)[:, None] * local_cols + iota(local_cols)[None, :])
    turns = source_cols[:, None, :] * held_k1[None, :, None] % length
    big_angle = turns.astype(jnp.float32) * (2.0 * math.pi / length)
    big_cos, big_sin = lax.optimization_barrier((jnp.cos(big_angle), jnp.sin(big_angle)))

    member_pieces = (
        [lefts[target // 2][target % 2] for target in range(entry_count)],
        [rights[target % 2][target % 2] for target in range(entry_count)],
        [rights[1 - target % 2][target % 2] for target in range(entry_count)],
    )
    entry_place = lax.axis_index("entry")
    block_rows = left_zero_zero.shape[0]
    block_outer = block_rows // (2 * row_count // RADIX)
    shift_of_slot = iota(row_count // (2 * row_count // RADIX)) // block_outer
    outer_index = ((entry_place - shift_of_slot) % entry_count) * block_outer + (
        iota(row_count // (2 * row_count // RADIX)) % block_outer
    )
    arrivals = []
    for pieces in member_pieces:
        stacked = digits(jnp.stack(pieces))
        blocks = [stacked[entry_place]]
        for shift in range(1, entry_count):
            pairs = [(place, (place + shift) % entry_count) for place in range(entry_count)]
            blocks.append(
                lax.ppermute(stacked[(entry_place + shift) % entry_count], "entry", pairs)
            )
        arrivals.append(jnp.concatenate(blocks, axis=0))
    spectra = []
    for arrived in arrivals:
        half_real, half_imag = column_half(arrived, outer_index)
        payload = jnp.stack([half_real, half_imag], axis=1)
        got = lax.all_to_all(payload, "fft", 0, 0, tiled=True)
        got_real = got[:, 0]
        got_imag = got[:, 1]
        packed = got_imag[:, 0:1]
        nyquist_row = jnp.where(on_first, packed, 0.0)
        got_imag = jnp.concatenate(
            [jnp.where(on_first, 0.0, packed), got_imag[:, 1:], jnp.zeros_like(packed)], axis=1
        )
        got_real = jnp.concatenate([got_real, nyquist_row], axis=1)
        got_real, got_imag = lax.optimization_barrier(
            rotate(got_real, got_imag, big_cos, -big_sin)
        )
        spectra.append(row_forward(got_real, got_imag, -1.0))

    sibling_pairs = [(place, place ^ 1) for place in range(entry_count)]
    sibling = lax.ppermute(jnp.stack(spectra[0]), "entry", sibling_pairs)
    head_real, head_imag = complex_product(*spectra[0], *spectra[1])
    rest_real, rest_imag = complex_product(sibling[0], sibling[1], *spectra[2])
    mixed_real = head_real + rest_real
    mixed_imag = head_imag + rest_imag
    part_rows = rows_here // 2
    pieces = (
        (slice(0, part_rows), True),
        (slice(part_rows, rows_here), False),
    )
    values = None
    nyquist = None
    for rows, with_nyquist in pieces:
        part_real = mixed_real[:, rows]
        part_imag = mixed_imag[:, rows]
        part_cos = big_cos[:, rows]
        part_sin = big_sin[:, rows]
        if with_nyquist:
            part_real = jnp.concatenate([part_real, mixed_real[:, rows_here:]], axis=1)
            part_imag = jnp.concatenate([part_imag, mixed_imag[:, rows_here:]], axis=1)
            part_cos = jnp.concatenate([part_cos, big_cos[:, rows_here:]], axis=1)
            part_sin = jnp.concatenate([part_sin, big_sin[:, rows_here:]], axis=1)
        back_real, back_imag = row_inverse(part_real, part_imag, 1.0)
        back_real, back_imag = rotate(back_real, back_imag, part_cos, part_sin)
        if with_nyquist:
            first_imag = jnp.where(on_first, back_real[:, part_rows:], back_imag[:, 0:1])
            back_imag = jnp.concatenate([first_imag, back_imag[:, 1:part_rows]], axis=1)
            back_real = back_real[:, :part_rows]
        payload = jnp.stack([back_real, back_imag], axis=1)
        got = lax.all_to_all(payload, "fft", 0, 0, tiled=True)
        full_real = got[:, 0]
        full_imag = got[:, 1]
        if with_nyquist:
            nyquist = full_imag[0, 0]
            full_real = full_real.at[0, 0].multiply(0.5)
            full_imag = full_imag.at[0, 0].set(0.0)
        part = column_part(full_real, full_imag, 2 * row_count, 1.0, rows.start)
        values = part if values is None else values + part
    alternating = (1 - 2 * (iota(2 * row_count) % 2)).astype(jnp.float32)
    values = 2.0 * values + alternating[:, None] * nyquist[None, :]
    out_scale = 1.0 / (length * math.sqrt(length // 2))
    return (values * out_scale)[None]


def solution(mesh):
    placed = (
        P("entry", "fft"),
        P("entry", "fft"),
        P("entry", "fft"),
        P("entry", "fft"),
        P("entry", "fft"),
        P("entry", "fft"),
        P("entry", "fft"),
        P("entry", "fft"),
    )
    return jax.shard_map(
        local, mesh=mesh, in_specs=placed, out_specs=P("entry", None, "fft"), check_vma=False
    )
```

```python
import math

import jax
import jax.numpy as jnp
from jax import lax
from jax.sharding import PartitionSpec as P

RADIX = 64


exact_precision = lax.Precision.HIGH


def contract(pattern, left_op, right_op):
    return jnp.einsum(
        pattern, left_op, right_op, precision=exact_precision, preferred_element_type=jnp.float32
    )


def iota(count):
    return jnp.arange(count, dtype=jnp.int32)


def angle_table(first_part, second_part, length, sense_sign):
    turns = first_part[:, None] * second_part[None, :] % length
    phase_angle = turns.astype(jnp.float32) * (2.0 * math.pi / length)
    return lax.optimization_barrier((jnp.cos(phase_angle), sense_sign * jnp.sin(phase_angle)))


def rotate(real_part, imag_part, cosine, sine):
    return (real_part * cosine - imag_part * sine, real_part * sine + imag_part * cosine)


def complex_product(left_real, left_imag, right_real, right_imag):
    return (
        left_real * right_real - left_imag * right_imag,
        left_real * right_imag + left_imag * right_real,
    )


def table_left(pattern, table, real_part, imag_part):
    cosine, sine = table
    if imag_part is None:
        return contract(pattern, cosine, real_part), contract(pattern, sine, real_part)
    return (
        contract(pattern, cosine, real_part) - contract(pattern, sine, imag_part),
        contract(pattern, sine, real_part) + contract(pattern, cosine, imag_part),
    )


def table_right(pattern, real_part, imag_part, table):
    cosine, sine = table
    return (
        contract(pattern, real_part, cosine) - contract(pattern, imag_part, sine),
        contract(pattern, real_part, sine) + contract(pattern, imag_part, cosine),
    )


def digits(limbs):
    return (limbs.astype(jnp.float32) - 32768.0) * (1.0 / 32768.0)


def column_half(values, outer_index):
    row_count, column_count = values.shape
    length = 2 * row_count
    inner_size = length // RADIX
    outer_count = row_count // inner_size
    first = angle_table(iota(RADIX), outer_index, RADIX, -1.0)
    flat = values.reshape(outer_count, inner_size * column_count)
    step_real, step_imag = table_left("ja,an->jn", first, flat, None)
    step_real = step_real.reshape(RADIX, inner_size, column_count)
    step_imag = step_imag.reshape(RADIX, inner_size, column_count)
    twist_cos, twist_sin = angle_table(iota(RADIX), iota(inner_size), length, -1.0)
    step_real, step_imag = lax.optimization_barrier(rotate(
        step_real, step_imag, twist_cos[:, :, None], twist_sin[:, :, None]
    ))
    second = angle_table(iota(inner_size // 2), iota(inner_size), inner_size, -1.0)
    final_real, final_imag = table_left("mb,jbc->mjc", second, step_real, step_imag)
    alternating = (1 - 2 * (iota(inner_size) % 2)).astype(jnp.float32)
    nyquist = contract("b,bc->c", alternating, step_real[0])
    final_imag = final_imag.at[0, 0].set(nyquist)
    return final_real, final_imag


def column_part(real_part, imag_part, length, sense_sign, offset):
    outer_count, part_size, column_count = real_part.shape
    inner_size = length // RADIX
    first = angle_table(iota(RADIX), iota(outer_count), RADIX, sense_sign)
    flat_real = real_part.reshape(outer_count, part_size * column_count)
    flat_imag = imag_part.reshape(outer_count, part_size * column_count)
    step_real, step_imag = table_left("ja,an->jn", first, flat_real, flat_imag)
    step_real = step_real.reshape(RADIX, part_size, column_count)
    step_imag = step_imag.reshape(RADIX, part_size, column_count)
    twist_cos, twist_sin = angle_table(iota(RADIX), offset + iota(part_size), length, sense_sign)
    step_real, step_imag = lax.optimization_barrier(rotate(
        step_real, step_imag, twist_cos[:, :, None], twist_sin[:, :, None]
    ))
    second_cos, second_sin = angle_table(iota(inner_size), offset + iota(part_size), inner_size, sense_sign)
    final_real = contract("mb,kbc->mkc", second_cos, step_real) - contract(
        "mb,kbc->mkc", second_sin, step_imag
    )
    return final_real.reshape(length, column_count)


def row_forward(real_part, imag_part, sense_sign):
    source_count, _, column_count = real_part.shape
    length = source_count * column_count
    first = angle_table(iota(source_count), iota(source_count), source_count, sense_sign)
    step_real, step_imag = table_left("us,src->urc", first, real_part, imag_part)
    twist_cos, twist_sin = angle_table(iota(source_count), iota(column_count), length, sense_sign)
    step_real, step_imag = rotate(
        step_real, step_imag, twist_cos[:, None, :], twist_sin[:, None, :]
    )
    second = angle_table(iota(column_count), iota(column_count), column_count, sense_sign)
    return table_right("urc,cv->urv", step_real, step_imag, second)


def row_inverse(real_part, imag_part, sense_sign):
    source_count, _, column_count = real_part.shape
    length = source_count * column_count
    second = angle_table(iota(column_count), iota(column_count), column_count, sense_sign)
    step_real, step_imag = table_right("urv,vc->urc", real_part, imag_part, second)
    twist_cos, twist_sin = angle_table(iota(source_count), iota(column_count), length, sense_sign)
    step_real, step_imag = rotate(
        step_real, step_imag, twist_cos[:, None, :], twist_sin[:, None, :]
    )
    first = angle_table(iota(source_count), iota(source_count), source_count, sense_sign)
    return table_left("su,urc->src", first, step_real, step_imag)


def local(
    left_zero_zero,
    left_zero_one,
    left_one_zero,
    left_one_one,
    right_zero_zero,
    right_zero_one,
    right_one_zero,
    right_one_one,
):
    lefts = [[left_zero_zero, left_zero_one], [left_one_zero, left_one_one]]
    rights = [[right_zero_zero, right_zero_one], [right_one_zero, right_one_one]]
    entry_count = lax.axis_size("entry")
    fft_count = lax.axis_size("fft")
    fft_place = lax.axis_index("fft")
    on_first = fft_place == 0
    local_cols = left_zero_zero.shape[1]
    row_count = left_zero_zero.shape[0] * entry_count
    length = 2 * row_count * local_cols * fft_count
    column_count = local_cols * fft_count
    rows_here = 2 * row_count // (2 * fft_count)

    held_k1 = jnp.concatenate(
        [fft_place * rows_here + iota(rows_here), jnp.full((1,), row_count, jnp.int32)]
    )
    source_cols = (iota(fft_count)[:, None] * local_cols + iota(local_cols)[None, :])
    turns = source_cols[:, None, :] * held_k1[None, :, None] % length
    big_angle = turns.astype(jnp.float32) * (2.0 * math.pi / length)
    big_cos, big_sin = lax.optimization_barrier((jnp.cos(big_angle), jnp.sin(big_angle)))

    member_pieces = (
        [lefts[target // 2][target % 2] for target in range(entry_count)],
        [rights[target % 2][target % 2] for target in range(entry_count)],
        [rights[1 - target % 2][target % 2] for target in range(entry_count)],
    )
    entry_place = lax.axis_index("entry")
    block_rows = left_zero_zero.shape[0]
    block_outer = block_rows // (2 * row_count // RADIX)
    shift_of_slot = iota(row_count // (2 * row_count // RADIX)) // block_outer
    outer_index = ((entry_place - shift_of_slot) % entry_count) * block_outer + (
        iota(row_count // (2 * row_count // RADIX)) % block_outer
    )
    arrivals = []
    for pieces in member_pieces:
        stacked = digits(jnp.stack(pieces))
        blocks = [stacked[entry_place]]
        for shift in range(1, entry_count):
            pairs = [(place, (place + shift) % entry_count) for place in range(entry_count)]
            blocks.append(
                lax.ppermute(stacked[(entry_place + shift) % entry_count], "entry", pairs)
            )
        arrivals.append(jnp.concatenate(blocks, axis=0))
    spectra = []
    for arrived in arrivals:
        half_real, half_imag = column_half(arrived, outer_index)
        payload = jnp.stack([half_real, half_imag], axis=1)
        got = lax.all_to_all(payload, "fft", 0, 0, tiled=True)
        got_real = got[:, 0]
        got_imag = got[:, 1]
        packed = got_imag[:, 0:1]
        nyquist_row = jnp.where(on_first, packed, 0.0)
        got_imag = jnp.concatenate(
            [jnp.where(on_first, 0.0, packed), got_imag[:, 1:], jnp.zeros_like(packed)], axis=1
        )
        got_real = jnp.concatenate([got_real, nyquist_row], axis=1)
        got_real, got_imag = lax.optimization_barrier(
            rotate(got_real, got_imag, big_cos, -big_sin)
        )
        spectra.append(row_forward(got_real, got_imag, -1.0))

    sibling_pairs = [(place, place ^ 1) for place in range(entry_count)]
    sibling = lax.ppermute(jnp.stack(spectra[0]), "entry", sibling_pairs)
    head_real, head_imag = complex_product(*spectra[0], *spectra[1])
    rest_real, rest_imag = complex_product(sibling[0], sibling[1], *spectra[2])
    mixed_real = head_real + rest_real
    mixed_imag = head_imag + rest_imag
    part_rows = rows_here // 2
    pieces = (
        (slice(0, part_rows), True),
        (slice(part_rows, rows_here), False),
    )
    values = None
    nyquist = None
    for rows, with_nyquist in pieces:
        part_real = mixed_real[:, rows]
        part_imag = mixed_imag[:, rows]
        part_cos = big_cos[:, rows]
        part_sin = big_sin[:, rows]
        if with_nyquist:
            part_real = jnp.concatenate([part_real, mixed_real[:, rows_here:]], axis=1)
            part_imag = jnp.concatenate([part_imag, mixed_imag[:, rows_here:]], axis=1)
            part_cos = jnp.concatenate([part_cos, big_cos[:, rows_here:]], axis=1)
            part_sin = jnp.concatenate([part_sin, big_sin[:, rows_here:]], axis=1)
        back_real, back_imag = row_inverse(part_real, part_imag, 1.0)
        back_real, back_imag = rotate(back_real, back_imag, part_cos, part_sin)
        if with_nyquist:
            first_imag = jnp.where(on_first, back_real[:, part_rows:], back_imag[:, 0:1])
            back_imag = jnp.concatenate([first_imag, back_imag[:, 1:part_rows]], axis=1)
            back_real = back_real[:, :part_rows]
        payload = jnp.stack([back_real, back_imag], axis=1)
        got = lax.all_to_all(payload, "fft", 0, 0, tiled=True)
        full_real = got[:, 0]
        full_imag = got[:, 1]
        if with_nyquist:
            nyquist = full_imag[0, 0]
            full_real = full_real.at[0, 0].multiply(0.5)
            full_imag = full_imag.at[0, 0].set(0.0)
        part = column_part(full_real, full_imag, 2 * row_count, 1.0, rows.start)
        values = part if values is None else values + part
    alternating = (1 - 2 * (iota(2 * row_count) % 2)).astype(jnp.float32)
    values = 2.0 * values + alternating[:, None] * nyquist[None, :]
    out_scale = 1.0 / (length * math.sqrt(length // 2))
    return (values * out_scale)[None]


def solution(mesh):
    placed = (
        P("entry", "fft"),
        P("entry", "fft"),
        P("entry", "fft"),
        P("entry", "fft"),
        P("entry", "fft"),
        P("entry", "fft"),
        P("entry", "fft"),
        P("entry", "fft"),
    )
    return jax.shard_map(
        local, mesh=mesh, in_specs=placed, out_specs=P("entry", None, "fft"), check_vma=False
    )
```

```python
import math

import jax
import jax.numpy as jnp
from jax import lax
from jax.sharding import PartitionSpec as P

RADIX = 64


exact_precision = lax.Precision.HIGHEST


def contract(pattern, left_op, right_op, precision=exact_precision):
    return jnp.einsum(
        pattern, left_op, right_op, precision=precision, preferred_element_type=jnp.float32
    )


def iota(count):
    return jnp.arange(count, dtype=jnp.int32)


def angle_table(first_part, second_part, length, sense_sign):
    turns = first_part[:, None] * second_part[None, :] % length
    phase_angle = turns.astype(jnp.float32) * (2.0 * math.pi / length)
    return lax.optimization_barrier((jnp.cos(phase_angle), sense_sign * jnp.sin(phase_angle)))


def rotate(real_part, imag_part, cosine, sine):
    return (real_part * cosine - imag_part * sine, real_part * sine + imag_part * cosine)


def complex_product(left_real, left_imag, right_real, right_imag):
    return (
        left_real * right_real - left_imag * right_imag,
        left_real * right_imag + left_imag * right_real,
    )


def table_left(pattern, table, real_part, imag_part):
    cosine, sine = table
    if imag_part is None:
        return contract(pattern, cosine, real_part), contract(pattern, sine, real_part)
    return (
        contract(pattern, cosine, real_part) - contract(pattern, sine, imag_part),
        contract(pattern, sine, real_part) + contract(pattern, cosine, imag_part),
    )


def table_right(pattern, real_part, imag_part, table, precision=exact_precision):
    cosine, sine = table
    return (
        contract(pattern, real_part, cosine, precision)
        - contract(pattern, imag_part, sine, precision),
        contract(pattern, real_part, sine, precision)
        + contract(pattern, imag_part, cosine, precision),
    )


def digits(limbs):
    return (limbs.astype(jnp.float32) - 32768.0) * (1.0 / 32768.0)


def column_half(values, outer_index):
    row_count, column_count = values.shape
    length = 2 * row_count
    inner_size = length // RADIX
    outer_count = row_count // inner_size
    first = angle_table(iota(RADIX), outer_index, RADIX, -1.0)
    flat = values.reshape(outer_count, inner_size * column_count)
    step_real, step_imag = table_left("ja,an->jn", first, flat, None)
    step_real = step_real.reshape(RADIX, inner_size, column_count)
    step_imag = step_imag.reshape(RADIX, inner_size, column_count)
    twist_cos, twist_sin = angle_table(iota(RADIX), iota(inner_size), length, -1.0)
    step_real, step_imag = lax.optimization_barrier(rotate(
        step_real, step_imag, twist_cos[:, :, None], twist_sin[:, :, None]
    ))
    second = angle_table(iota(inner_size // 2), iota(inner_size), inner_size, -1.0)
    final_real, final_imag = table_left("mb,jbc->mjc", second, step_real, step_imag)
    alternating = (1 - 2 * (iota(inner_size) % 2)).astype(jnp.float32)
    nyquist = contract("b,bc->c", alternating, step_real[0])
    final_imag = final_imag.at[0, 0].set(nyquist)
    return final_real, final_imag


def column_part(real_part, imag_part, length, sense_sign, offset):
    outer_count, part_size, column_count = real_part.shape
    inner_size = length // RADIX
    first = angle_table(iota(RADIX), iota(outer_count), RADIX, sense_sign)
    flat_real = real_part.reshape(outer_count, part_size * column_count)
    flat_imag = imag_part.reshape(outer_count, part_size * column_count)
    step_real, step_imag = table_left("ja,an->jn", first, flat_real, flat_imag)
    step_real = step_real.reshape(RADIX, part_size, column_count)
    step_imag = step_imag.reshape(RADIX, part_size, column_count)
    twist_cos, twist_sin = angle_table(iota(RADIX), offset + iota(part_size), length, sense_sign)
    step_real, step_imag = lax.optimization_barrier(rotate(
        step_real, step_imag, twist_cos[:, :, None], twist_sin[:, :, None]
    ))
    second_cos, second_sin = angle_table(iota(inner_size), offset + iota(part_size), inner_size, sense_sign)
    final_real = contract("mb,kbc->mkc", second_cos, step_real) - contract(
        "mb,kbc->mkc", second_sin, step_imag
    )
    return final_real.reshape(length, column_count)


def row_forward(real_part, imag_part, sense_sign):
    source_count, _, column_count = real_part.shape
    length = source_count * column_count
    first = angle_table(iota(source_count), iota(source_count), source_count, sense_sign)
    step_real, step_imag = table_left("us,src->urc", first, real_part, imag_part)
    twist_cos, twist_sin = angle_table(iota(source_count), iota(column_count), length, sense_sign)
    step_real, step_imag = rotate(
        step_real, step_imag, twist_cos[:, None, :], twist_sin[:, None, :]
    )
    second = angle_table(iota(column_count), iota(column_count), column_count, sense_sign)
    return table_right("urc,cv->urv", step_real, step_imag, second, lax.Precision.HIGH)


def row_inverse(real_part, imag_part, sense_sign):
    source_count, _, column_count = real_part.shape
    length = source_count * column_count
    second = angle_table(iota(column_count), iota(column_count), column_count, sense_sign)
    step_real, step_imag = table_right(
        "urv,vc->urc", real_part, imag_part, second, lax.Precision.HIGH
    )
    twist_cos, twist_sin = angle_table(iota(source_count), iota(column_count), length, sense_sign)
    step_real, step_imag = rotate(
        step_real, step_imag, twist_cos[:, None, :], twist_sin[:, None, :]
    )
    first = angle_table(iota(source_count), iota(source_count), source_count, sense_sign)
    return table_left("su,urc->src", first, step_real, step_imag)


def local(
    left_zero_zero,
    left_zero_one,
    left_one_zero,
    left_one_one,
    right_zero_zero,
    right_zero_one,
    right_one_zero,
    right_one_one,
):
    lefts = [[left_zero_zero, left_zero_one], [left_one_zero, left_one_one]]
    rights = [[right_zero_zero, right_zero_one], [right_one_zero, right_one_one]]
    entry_count = lax.axis_size("entry")
    fft_count = lax.axis_size("fft")
    fft_place = lax.axis_index("fft")
    on_first = fft_place == 0
    local_cols = left_zero_zero.shape[1]
    row_count = left_zero_zero.shape[0] * entry_count
    length = 2 * row_count * local_cols * fft_count
    column_count = local_cols * fft_count
    rows_here = 2 * row_count // (2 * fft_count)

    held_k1 = jnp.concatenate(
        [fft_place * rows_here + iota(rows_here), jnp.full((1,), row_count, jnp.int32)]
    )
    source_cols = (iota(fft_count)[:, None] * local_cols + iota(local_cols)[None, :])
    turns = source_cols[:, None, :] * held_k1[None, :, None] % length
    big_angle = turns.astype(jnp.float32) * (2.0 * math.pi / length)
    big_cos, big_sin = lax.optimization_barrier((jnp.cos(big_angle), jnp.sin(big_angle)))

    member_pieces = (
        [lefts[target // 2][target % 2] for target in range(entry_count)],
        [rights[target % 2][target % 2] for target in range(entry_count)],
        [rights[1 - target % 2][target % 2] for target in range(entry_count)],
    )
    entry_place = lax.axis_index("entry")
    block_rows = left_zero_zero.shape[0]
    block_outer = block_rows // (2 * row_count // RADIX)
    shift_of_slot = iota(row_count // (2 * row_count // RADIX)) // block_outer
    outer_index = ((entry_place - shift_of_slot) % entry_count) * block_outer + (
        iota(row_count // (2 * row_count // RADIX)) % block_outer
    )
    arrivals = []
    for pieces in member_pieces:
        stacked = digits(jnp.stack(pieces))
        blocks = [stacked[entry_place]]
        for shift in range(1, entry_count):
            pairs = [(place, (place + shift) % entry_count) for place in range(entry_count)]
            blocks.append(
                lax.ppermute(stacked[(entry_place + shift) % entry_count], "entry", pairs)
            )
        arrivals.append(jnp.concatenate(blocks, axis=0))
    spectra = []
    for arrived in arrivals:
        half_real, half_imag = column_half(arrived, outer_index)
        payload = jnp.stack([half_real, half_imag], axis=1)
        got = lax.all_to_all(payload, "fft", 0, 0, tiled=True)
        got_real = got[:, 0]
        got_imag = got[:, 1]
        packed = got_imag[:, 0:1]
        nyquist_row = jnp.where(on_first, packed, 0.0)
        got_imag = jnp.concatenate(
            [jnp.where(on_first, 0.0, packed), got_imag[:, 1:], jnp.zeros_like(packed)], axis=1
        )
        got_real = jnp.concatenate([got_real, nyquist_row], axis=1)
        got_real, got_imag = lax.optimization_barrier(
            rotate(got_real, got_imag, big_cos, -big_sin)
        )
        spectra.append(row_forward(got_real, got_imag, -1.0))

    sibling_pairs = [(place, place ^ 1) for place in range(entry_count)]
    sibling = lax.ppermute(jnp.stack(spectra[0]), "entry", sibling_pairs)
    head_real, head_imag = complex_product(*spectra[0], *spectra[1])
    rest_real, rest_imag = complex_product(sibling[0], sibling[1], *spectra[2])
    mixed_real = head_real + rest_real
    mixed_imag = head_imag + rest_imag
    part_rows = rows_here // 2
    pieces = (
        (slice(0, part_rows), True),
        (slice(part_rows, rows_here), False),
    )
    values = None
    nyquist = None
    for rows, with_nyquist in pieces:
        part_real = mixed_real[:, rows]
        part_imag = mixed_imag[:, rows]
        part_cos = big_cos[:, rows]
        part_sin = big_sin[:, rows]
        if with_nyquist:
            part_real = jnp.concatenate([part_real, mixed_real[:, rows_here:]], axis=1)
            part_imag = jnp.concatenate([part_imag, mixed_imag[:, rows_here:]], axis=1)
            part_cos = jnp.concatenate([part_cos, big_cos[:, rows_here:]], axis=1)
            part_sin = jnp.concatenate([part_sin, big_sin[:, rows_here:]], axis=1)
        back_real, back_imag = row_inverse(part_real, part_imag, 1.0)
        back_real, back_imag = rotate(back_real, back_imag, part_cos, part_sin)
        if with_nyquist:
            first_imag = jnp.where(on_first, back_real[:, part_rows:], back_imag[:, 0:1])
            back_imag = jnp.concatenate([first_imag, back_imag[:, 1:part_rows]], axis=1)
            back_real = back_real[:, :part_rows]
        payload = jnp.stack([back_real, back_imag], axis=1)
        got = lax.all_to_all(payload, "fft", 0, 0, tiled=True)
        full_real = got[:, 0]
        full_imag = got[:, 1]
        if with_nyquist:
            nyquist = full_imag[0, 0]
            full_real = full_real.at[0, 0].multiply(0.5)
            full_imag = full_imag.at[0, 0].set(0.0)
        part = column_part(full_real, full_imag, 2 * row_count, 1.0, rows.start)
        values = part if values is None else values + part
    alternating = (1 - 2 * (iota(2 * row_count) % 2)).astype(jnp.float32)
    values = 2.0 * values + alternating[:, None] * nyquist[None, :]
    out_scale = 1.0 / (length * math.sqrt(length // 2))
    return (values * out_scale)[None]


def solution(mesh):
    placed = (
        P("entry", "fft"),
        P("entry", "fft"),
        P("entry", "fft"),
        P("entry", "fft"),
        P("entry", "fft"),
        P("entry", "fft"),
        P("entry", "fft"),
        P("entry", "fft"),
    )
    return jax.shard_map(
        local, mesh=mesh, in_specs=placed, out_specs=P("entry", None, "fft"), check_vma=False
    )
```

```python
import math

import jax
import jax.numpy as jnp
from jax import lax
from jax.sharding import PartitionSpec as P

RADIX = 64


exact_precision = lax.Precision.HIGHEST


def contract(pattern, left_op, right_op, precision=exact_precision):
    return jnp.einsum(
        pattern, left_op, right_op, precision=precision, preferred_element_type=jnp.float32
    )


def iota(count):
    return jnp.arange(count, dtype=jnp.int32)


def angle_table(first_part, second_part, length, sense_sign):
    turns = first_part[:, None] * second_part[None, :] % length
    phase_angle = turns.astype(jnp.float32) * (2.0 * math.pi / length)
    return lax.optimization_barrier((jnp.cos(phase_angle), sense_sign * jnp.sin(phase_angle)))


def rotate(real_part, imag_part, cosine, sine):
    return (real_part * cosine - imag_part * sine, real_part * sine + imag_part * cosine)


def complex_product(left_real, left_imag, right_real, right_imag):
    return (
        left_real * right_real - left_imag * right_imag,
        left_real * right_imag + left_imag * right_real,
    )


def table_left(pattern, table, real_part, imag_part):
    cosine, sine = table
    if imag_part is None:
        return contract(pattern, cosine, real_part), contract(pattern, sine, real_part)
    return (
        contract(pattern, cosine, real_part) - contract(pattern, sine, imag_part),
        contract(pattern, sine, real_part) + contract(pattern, cosine, imag_part),
    )


def table_right(pattern, real_part, imag_part, table, precision=exact_precision):
    cosine, sine = table
    return (
        contract(pattern, real_part, cosine, precision)
        - contract(pattern, imag_part, sine, precision),
        contract(pattern, real_part, sine, precision)
        + contract(pattern, imag_part, cosine, precision),
    )


def digits(limbs):
    return (limbs.astype(jnp.float32) - 32768.0) * (1.0 / 32768.0)


def column_half(values, outer_index):
    row_count, column_count = values.shape
    length = 2 * row_count
    inner_size = length // RADIX
    outer_count = row_count // inner_size
    first = angle_table(iota(RADIX), outer_index, RADIX, -1.0)
    flat = values.reshape(outer_count, inner_size * column_count)
    step_real, step_imag = table_left("ja,an->jn", first, flat, None)
    step_real = step_real.reshape(RADIX, inner_size, column_count)
    step_imag = step_imag.reshape(RADIX, inner_size, column_count)
    twist_cos, twist_sin = angle_table(iota(RADIX), iota(inner_size), length, -1.0)
    step_real, step_imag = lax.optimization_barrier(rotate(
        step_real, step_imag, twist_cos[:, :, None], twist_sin[:, :, None]
    ))
    second = angle_table(iota(inner_size // 2), iota(inner_size), inner_size, -1.0)
    final_real, final_imag = table_left("mb,jbc->mjc", second, step_real, step_imag)
    alternating = (1 - 2 * (iota(inner_size) % 2)).astype(jnp.float32)
    nyquist = contract("b,bc->c", alternating, step_real[0])
    final_imag = final_imag.at[0, 0].set(nyquist)
    return final_real, final_imag


def column_part(real_part, imag_part, length, sense_sign, offset):
    outer_count, part_size, column_count = real_part.shape
    inner_size = length // RADIX
    first = angle_table(iota(RADIX), iota(outer_count), RADIX, sense_sign)
    flat_real = real_part.reshape(outer_count, part_size * column_count)
    flat_imag = imag_part.reshape(outer_count, part_size * column_count)
    step_real, step_imag = table_left("ja,an->jn", first, flat_real, flat_imag)
    step_real = step_real.reshape(RADIX, part_size, column_count)
    step_imag = step_imag.reshape(RADIX, part_size, column_count)
    twist_cos, twist_sin = angle_table(iota(RADIX), offset + iota(part_size), length, sense_sign)
    step_real, step_imag = lax.optimization_barrier(rotate(
        step_real, step_imag, twist_cos[:, :, None], twist_sin[:, :, None]
    ))
    second_cos, second_sin = angle_table(iota(inner_size), offset + iota(part_size), inner_size, sense_sign)
    final_real = contract("mb,kbc->mkc", second_cos, step_real) - contract(
        "mb,kbc->mkc", second_sin, step_imag
    )
    return final_real.reshape(length, column_count)


def row_forward(real_part, imag_part, sense_sign):
    source_count, _, column_count = real_part.shape
    length = source_count * column_count
    first = angle_table(iota(source_count), iota(source_count), source_count, sense_sign)
    step_real, step_imag = table_left("us,src->urc", first, real_part, imag_part)
    twist_cos, twist_sin = angle_table(iota(source_count), iota(column_count), length, sense_sign)
    step_real, step_imag = rotate(
        step_real, step_imag, twist_cos[:, None, :], twist_sin[:, None, :]
    )
    second = angle_table(iota(column_count), iota(column_count), column_count, sense_sign)
    return table_right("urc,cv->urv", step_real, step_imag, second, lax.Precision.HIGH)


def row_inverse(real_part, imag_part, sense_sign):
    source_count, _, column_count = real_part.shape
    length = source_count * column_count
    second = angle_table(iota(column_count), iota(column_count), column_count, sense_sign)
    step_real, step_imag = table_right(
        "urv,vc->urc", real_part, imag_part, second, lax.Precision.HIGH
    )
    twist_cos, twist_sin = angle_table(iota(source_count), iota(column_count), length, sense_sign)
    step_real, step_imag = rotate(
        step_real, step_imag, twist_cos[:, None, :], twist_sin[:, None, :]
    )
    first = angle_table(iota(source_count), iota(source_count), source_count, sense_sign)
    return table_left("su,urc->src", first, step_real, step_imag)


def local(
    left_zero_zero,
    left_zero_one,
    left_one_zero,
    left_one_one,
    right_zero_zero,
    right_zero_one,
    right_one_zero,
    right_one_one,
):
    lefts = [[left_zero_zero, left_zero_one], [left_one_zero, left_one_one]]
    rights = [[right_zero_zero, right_zero_one], [right_one_zero, right_one_one]]
    entry_count = lax.axis_size("entry")
    fft_count = lax.axis_size("fft")
    fft_place = lax.axis_index("fft")
    on_first = fft_place == 0
    local_cols = left_zero_zero.shape[1]
    row_count = left_zero_zero.shape[0] * entry_count
    length = 2 * row_count * local_cols * fft_count
    column_count = local_cols * fft_count
    rows_here = 2 * row_count // (2 * fft_count)

    held_k1 = jnp.concatenate(
        [fft_place * rows_here + iota(rows_here), jnp.full((1,), row_count, jnp.int32)]
    )
    source_cols = (iota(fft_count)[:, None] * local_cols + iota(local_cols)[None, :])
    turns = source_cols[:, None, :] * held_k1[None, :, None] % length
    big_angle = turns.astype(jnp.float32) * (2.0 * math.pi / length)
    big_cos, big_sin = lax.optimization_barrier((jnp.cos(big_angle), jnp.sin(big_angle)))

    member_pieces = (
        [lefts[target // 2][target % 2] for target in range(entry_count)],
        [rights[target % 2][target % 2] for target in range(entry_count)],
        [rights[1 - target % 2][target % 2] for target in range(entry_count)],
    )
    entry_place = lax.axis_index("entry")
    block_rows = left_zero_zero.shape[0]
    block_outer = block_rows // (2 * row_count // RADIX)
    shift_of_slot = iota(row_count // (2 * row_count // RADIX)) // block_outer
    outer_index = ((entry_place - shift_of_slot) % entry_count) * block_outer + (
        iota(row_count // (2 * row_count // RADIX)) % block_outer
    )
    def exchanged(stacked):
        blocks = [stacked[entry_place]]
        for shift in range(1, entry_count):
            pairs = [(place, (place + shift) % entry_count) for place in range(entry_count)]
            blocks.append(
                lax.ppermute(stacked[(entry_place + shift) % entry_count], "entry", pairs)
            )
        return jnp.concatenate(blocks, axis=0)

    outgoing = [digits(jnp.stack(pieces)) for pieces in member_pieces]
    spectra = []
    for member in range(len(outgoing)):
        half_real, half_imag = column_half(exchanged(outgoing[member]), outer_index)
        payload = jnp.stack([half_real, half_imag], axis=1)
        if member == 0:
            payload, *rest = lax.optimization_barrier((payload, *outgoing[1:]))
            outgoing[1:] = rest
        got = lax.all_to_all(payload, "fft", 0, 0, tiled=True)
        got_real = got[:, 0]
        got_imag = got[:, 1]
        packed = got_imag[:, 0:1]
        nyquist_row = jnp.where(on_first, packed, 0.0)
        got_imag = jnp.concatenate(
            [jnp.where(on_first, 0.0, packed), got_imag[:, 1:], jnp.zeros_like(packed)], axis=1
        )
        got_real = jnp.concatenate([got_real, nyquist_row], axis=1)
        got_real, got_imag = lax.optimization_barrier(
            rotate(got_real, got_imag, big_cos, -big_sin)
        )
        spectra.append(row_forward(got_real, got_imag, -1.0))

    sibling_pairs = [(place, place ^ 1) for place in range(entry_count)]
    sibling = lax.ppermute(jnp.stack(spectra[0]), "entry", sibling_pairs)
    head_real, head_imag = complex_product(*spectra[0], *spectra[1])
    rest_real, rest_imag = complex_product(sibling[0], sibling[1], *spectra[2])
    mixed_real = head_real + rest_real
    mixed_imag = head_imag + rest_imag
    part_rows = rows_here // 2
    pieces = (
        (slice(0, part_rows), True),
        (slice(part_rows, rows_here), False),
    )
    values = None
    nyquist = None
    for rows, with_nyquist in pieces:
        part_real = mixed_real[:, rows]
        part_imag = mixed_imag[:, rows]
        part_cos = big_cos[:, rows]
        part_sin = big_sin[:, rows]
        if with_nyquist:
            part_real = jnp.concatenate([part_real, mixed_real[:, rows_here:]], axis=1)
            part_imag = jnp.concatenate([part_imag, mixed_imag[:, rows_here:]], axis=1)
            part_cos = jnp.concatenate([part_cos, big_cos[:, rows_here:]], axis=1)
            part_sin = jnp.concatenate([part_sin, big_sin[:, rows_here:]], axis=1)
        back_real, back_imag = row_inverse(part_real, part_imag, 1.0)
        back_real, back_imag = rotate(back_real, back_imag, part_cos, part_sin)
        if with_nyquist:
            first_imag = jnp.where(on_first, back_real[:, part_rows:], back_imag[:, 0:1])
            back_imag = jnp.concatenate([first_imag, back_imag[:, 1:part_rows]], axis=1)
            back_real = back_real[:, :part_rows]
        payload = jnp.stack([back_real, back_imag], axis=1)
        got = lax.all_to_all(payload, "fft", 0, 0, tiled=True)
        full_real = got[:, 0]
        full_imag = got[:, 1]
        if with_nyquist:
            nyquist = full_imag[0, 0]
            full_real = full_real.at[0, 0].multiply(0.5)
            full_imag = full_imag.at[0, 0].set(0.0)
        part = column_part(full_real, full_imag, 2 * row_count, 1.0, rows.start)
        values = part if values is None else values + part
    alternating = (1 - 2 * (iota(2 * row_count) % 2)).astype(jnp.float32)
    values = 2.0 * values + alternating[:, None] * nyquist[None, :]
    out_scale = 1.0 / (length * math.sqrt(length // 2))
    return (values * out_scale)[None]


def solution(mesh):
    placed = (
        P("entry", "fft"),
        P("entry", "fft"),
        P("entry", "fft"),
        P("entry", "fft"),
        P("entry", "fft"),
        P("entry", "fft"),
        P("entry", "fft"),
        P("entry", "fft"),
    )
    return jax.shard_map(
        local, mesh=mesh, in_specs=placed, out_specs=P("entry", None, "fft"), check_vma=False
    )
```

```python
import math

import jax
import jax.numpy as jnp
from jax import lax
from jax.sharding import PartitionSpec as P

RADIX = 64


exact_precision = lax.Precision.HIGHEST


def contract(pattern, left_op, right_op, precision=exact_precision):
    return jnp.einsum(
        pattern, left_op, right_op, precision=precision, preferred_element_type=jnp.float32
    )


def iota(count):
    return jnp.arange(count, dtype=jnp.int32)


def angle_table(first_part, second_part, length, sense_sign):
    turns = first_part[:, None] * second_part[None, :] % length
    phase_angle = turns.astype(jnp.float32) * (2.0 * math.pi / length)
    return lax.optimization_barrier((jnp.cos(phase_angle), sense_sign * jnp.sin(phase_angle)))


def rotate(real_part, imag_part, cosine, sine):
    return (real_part * cosine - imag_part * sine, real_part * sine + imag_part * cosine)


def complex_product(left_real, left_imag, right_real, right_imag):
    return (
        left_real * right_real - left_imag * right_imag,
        left_real * right_imag + left_imag * right_real,
    )


def table_left(pattern, table, real_part, imag_part):
    cosine, sine = table
    if imag_part is None:
        return contract(pattern, cosine, real_part), contract(pattern, sine, real_part)
    return (
        contract(pattern, cosine, real_part) - contract(pattern, sine, imag_part),
        contract(pattern, sine, real_part) + contract(pattern, cosine, imag_part),
    )


def table_right(pattern, real_part, imag_part, table, precision=exact_precision):
    cosine, sine = table
    return (
        contract(pattern, real_part, cosine, precision)
        - contract(pattern, imag_part, sine, precision),
        contract(pattern, real_part, sine, precision)
        + contract(pattern, imag_part, cosine, precision),
    )


def digits(limbs):
    return (limbs.astype(jnp.float32) - 32768.0) * (1.0 / 32768.0)


def column_half(values, outer_index):
    row_count, column_count = values.shape
    length = 2 * row_count
    inner_size = length // RADIX
    outer_count = row_count // inner_size
    first = angle_table(iota(RADIX), outer_index, RADIX, -1.0)
    flat = values.reshape(outer_count, inner_size * column_count)
    step_real, step_imag = table_left("ja,an->jn", first, flat, None)
    step_real = step_real.reshape(RADIX, inner_size, column_count)
    step_imag = step_imag.reshape(RADIX, inner_size, column_count)
    twist_cos, twist_sin = angle_table(iota(RADIX), iota(inner_size), length, -1.0)
    step_real, step_imag = lax.optimization_barrier(rotate(
        step_real, step_imag, twist_cos[:, :, None], twist_sin[:, :, None]
    ))
    second = angle_table(iota(inner_size // 2), iota(inner_size), inner_size, -1.0)
    final_real, final_imag = table_left("mb,jbc->mjc", second, step_real, step_imag)
    alternating = (1 - 2 * (iota(inner_size) % 2)).astype(jnp.float32)
    nyquist = contract("b,bc->c", alternating, step_real[0])
    final_imag = final_imag.at[0, 0].set(nyquist)
    return final_real, final_imag


def column_part(real_part, imag_part, length, sense_sign, offset):
    outer_count, part_size, column_count = real_part.shape
    inner_size = length // RADIX
    first = angle_table(iota(RADIX), iota(outer_count), RADIX, sense_sign)
    flat_real = real_part.reshape(outer_count, part_size * column_count)
    flat_imag = imag_part.reshape(outer_count, part_size * column_count)
    step_real, step_imag = table_left("ja,an->jn", first, flat_real, flat_imag)
    step_real = step_real.reshape(RADIX, part_size, column_count)
    step_imag = step_imag.reshape(RADIX, part_size, column_count)
    twist_cos, twist_sin = angle_table(iota(RADIX), offset + iota(part_size), length, sense_sign)
    step_real, step_imag = lax.optimization_barrier(rotate(
        step_real, step_imag, twist_cos[:, :, None], twist_sin[:, :, None]
    ))
    second_cos, second_sin = angle_table(iota(inner_size), offset + iota(part_size), inner_size, sense_sign)
    final_real = contract("mb,kbc->mkc", second_cos, step_real) - contract(
        "mb,kbc->mkc", second_sin, step_imag
    )
    return final_real.reshape(length, column_count)


def row_forward(real_part, imag_part, sense_sign):
    source_count, _, column_count = real_part.shape
    length = source_count * column_count
    first = angle_table(iota(source_count), iota(source_count), source_count, sense_sign)
    step_real, step_imag = table_left("us,src->urc", first, real_part, imag_part)
    twist_cos, twist_sin = angle_table(iota(source_count), iota(column_count), length, sense_sign)
    step_real, step_imag = rotate(
        step_real, step_imag, twist_cos[:, None, :], twist_sin[:, None, :]
    )
    second = angle_table(iota(column_count), iota(column_count), column_count, sense_sign)
    return table_right("urc,cv->urv", step_real, step_imag, second, lax.Precision.HIGH)


def row_inverse(real_part, imag_part, sense_sign):
    source_count, _, column_count = real_part.shape
    length = source_count * column_count
    second = angle_table(iota(column_count), iota(column_count), column_count, sense_sign)
    step_real, step_imag = table_right(
        "urv,vc->urc", real_part, imag_part, second, lax.Precision.HIGH
    )
    twist_cos, twist_sin = angle_table(iota(source_count), iota(column_count), length, sense_sign)
    step_real, step_imag = rotate(
        step_real, step_imag, twist_cos[:, None, :], twist_sin[:, None, :]
    )
    first = angle_table(iota(source_count), iota(source_count), source_count, sense_sign)
    return table_left("su,urc->src", first, step_real, step_imag)


def local(
    left_zero_zero,
    left_zero_one,
    left_one_zero,
    left_one_one,
    right_zero_zero,
    right_zero_one,
    right_one_zero,
    right_one_one,
):
    lefts = [[left_zero_zero, left_zero_one], [left_one_zero, left_one_one]]
    rights = [[right_zero_zero, right_zero_one], [right_one_zero, right_one_one]]
    entry_count = lax.axis_size("entry")
    fft_count = lax.axis_size("fft")
    fft_place = lax.axis_index("fft")
    on_first = fft_place == 0
    local_cols = left_zero_zero.shape[1]
    row_count = left_zero_zero.shape[0] * entry_count
    length = 2 * row_count * local_cols * fft_count
    column_count = local_cols * fft_count
    rows_here = 2 * row_count // (2 * fft_count)

    held_k1 = jnp.concatenate(
        [fft_place * rows_here + iota(rows_here), jnp.full((1,), row_count, jnp.int32)]
    )
    source_cols = (iota(fft_count)[:, None] * local_cols + iota(local_cols)[None, :])
    turns = source_cols[:, None, :] * held_k1[None, :, None] % length
    big_angle = turns.astype(jnp.float32) * (2.0 * math.pi / length)
    big_cos, big_sin = lax.optimization_barrier((jnp.cos(big_angle), jnp.sin(big_angle)))

    member_pieces = (
        [
            rights[target % 2][target % 2] if target // 2 == 0 else rights[1 - target % 2][target % 2]
            for target in range(entry_count)
        ],
        [lefts[target // 2][target % 2] for target in range(entry_count)],
    )
    entry_place = lax.axis_index("entry")
    block_rows = left_zero_zero.shape[0]
    block_outer = block_rows // (2 * row_count // RADIX)
    shift_of_slot = iota(row_count // (2 * row_count // RADIX)) // block_outer
    outer_index = ((entry_place - shift_of_slot) % entry_count) * block_outer + (
        iota(row_count // (2 * row_count // RADIX)) % block_outer
    )
    arrivals = []
    for pieces in member_pieces:
        stacked = digits(jnp.stack(pieces))
        blocks = [stacked[entry_place]]
        for shift in range(1, entry_count):
            pairs = [(place, (place + shift) % entry_count) for place in range(entry_count)]
            blocks.append(
                lax.ppermute(stacked[(entry_place + shift) % entry_count], "entry", pairs)
            )
        arrivals.append(jnp.concatenate(blocks, axis=0))
    spectra = []
    for arrived in arrivals:
        half_real, half_imag = column_half(arrived, outer_index)
        payload = jnp.stack([half_real, half_imag], axis=1)
        got = lax.all_to_all(payload, "fft", 0, 0, tiled=True)
        got_real = got[:, 0]
        got_imag = got[:, 1]
        packed = got_imag[:, 0:1]
        nyquist_row = jnp.where(on_first, packed, 0.0)
        got_imag = jnp.concatenate(
            [jnp.where(on_first, 0.0, packed), got_imag[:, 1:], jnp.zeros_like(packed)], axis=1
        )
        got_real = jnp.concatenate([got_real, nyquist_row], axis=1)
        got_real, got_imag = lax.optimization_barrier(
            rotate(got_real, got_imag, big_cos, -big_sin)
        )
        spectra.append(row_forward(got_real, got_imag, -1.0))

    mine, own = spectra
    other = lax.ppermute(jnp.stack(mine), "entry", [(place, place ^ 2) for place in range(entry_count)])
    sibling = lax.ppermute(jnp.stack(own), "entry", [(place, place ^ 1) for place in range(entry_count)])
    upper = entry_place // 2 == 0
    pair_real = jnp.where(upper, own[0], sibling[0])
    pair_imag = jnp.where(upper, own[1], sibling[1])
    rest_a_real = jnp.where(upper, sibling[0], own[0])
    rest_a_imag = jnp.where(upper, sibling[1], own[1])
    head_real, head_imag = complex_product(pair_real, pair_imag, *mine)
    rest_real, rest_imag = complex_product(rest_a_real, rest_a_imag, other[0], other[1])
    mixed_real = head_real + rest_real
    mixed_imag = head_imag + rest_imag
    part_rows = rows_here // 2
    pieces = (
        (slice(0, part_rows), True),
        (slice(part_rows, rows_here), False),
    )
    values = None
    nyquist = None
    for rows, with_nyquist in pieces:
        part_real = mixed_real[:, rows]
        part_imag = mixed_imag[:, rows]
        part_cos = big_cos[:, rows]
        part_sin = big_sin[:, rows]
        if with_nyquist:
            part_real = jnp.concatenate([part_real, mixed_real[:, rows_here:]], axis=1)
            part_imag = jnp.concatenate([part_imag, mixed_imag[:, rows_here:]], axis=1)
            part_cos = jnp.concatenate([part_cos, big_cos[:, rows_here:]], axis=1)
            part_sin = jnp.concatenate([part_sin, big_sin[:, rows_here:]], axis=1)
        back_real, back_imag = row_inverse(part_real, part_imag, 1.0)
        back_real, back_imag = rotate(back_real, back_imag, part_cos, part_sin)
        if with_nyquist:
            first_imag = jnp.where(on_first, back_real[:, part_rows:], back_imag[:, 0:1])
            back_imag = jnp.concatenate([first_imag, back_imag[:, 1:part_rows]], axis=1)
            back_real = back_real[:, :part_rows]
        payload = jnp.stack([back_real, back_imag], axis=1)
        got = lax.all_to_all(payload, "fft", 0, 0, tiled=True)
        full_real = got[:, 0]
        full_imag = got[:, 1]
        if with_nyquist:
            nyquist = full_imag[0, 0]
            full_real = full_real.at[0, 0].multiply(0.5)
            full_imag = full_imag.at[0, 0].set(0.0)
        part = column_part(full_real, full_imag, 2 * row_count, 1.0, rows.start)
        values = part if values is None else values + part
    alternating = (1 - 2 * (iota(2 * row_count) % 2)).astype(jnp.float32)
    values = 2.0 * values + alternating[:, None] * nyquist[None, :]
    out_scale = 1.0 / (length * math.sqrt(length // 2))
    return (values * out_scale)[None]


def solution(mesh):
    placed = (
        P("entry", "fft"),
        P("entry", "fft"),
        P("entry", "fft"),
        P("entry", "fft"),
        P("entry", "fft"),
        P("entry", "fft"),
        P("entry", "fft"),
        P("entry", "fft"),
    )
    return jax.shard_map(
        local, mesh=mesh, in_specs=placed, out_specs=P("entry", None, "fft"), check_vma=False
    )
```

```python
import math

import jax
import jax.numpy as jnp
from jax import lax
from jax.sharding import PartitionSpec as P

RADIX = 64


exact_precision = lax.Precision.HIGHEST


def contract(pattern, left_op, right_op, precision=exact_precision):
    return jnp.einsum(
        pattern, left_op, right_op, precision=precision, preferred_element_type=jnp.float32
    )


def iota(count):
    return jnp.arange(count, dtype=jnp.int32)


def angle_table(first_part, second_part, length, sense_sign):
    turns = first_part[:, None] * second_part[None, :] % length
    phase_angle = turns.astype(jnp.float32) * (2.0 * math.pi / length)
    return lax.optimization_barrier((jnp.cos(phase_angle), sense_sign * jnp.sin(phase_angle)))


def rotate(real_part, imag_part, cosine, sine):
    return (real_part * cosine - imag_part * sine, real_part * sine + imag_part * cosine)


def complex_product(left_real, left_imag, right_real, right_imag):
    return (
        left_real * right_real - left_imag * right_imag,
        left_real * right_imag + left_imag * right_real,
    )


def table_left(pattern, table, real_part, imag_part):
    cosine, sine = table
    if imag_part is None:
        return contract(pattern, cosine, real_part), contract(pattern, sine, real_part)
    return (
        contract(pattern, cosine, real_part) - contract(pattern, sine, imag_part),
        contract(pattern, sine, real_part) + contract(pattern, cosine, imag_part),
    )


def table_right(pattern, real_part, imag_part, table, precision=exact_precision):
    cosine, sine = table
    return (
        contract(pattern, real_part, cosine, precision)
        - contract(pattern, imag_part, sine, precision),
        contract(pattern, real_part, sine, precision)
        + contract(pattern, imag_part, cosine, precision),
    )


def digits(limbs):
    return (limbs.astype(jnp.float32) - 32768.0) * (1.0 / 32768.0)


def column_half(values, outer_index):
    row_count, column_count = values.shape
    length = 2 * row_count
    inner_size = length // RADIX
    outer_count = row_count // inner_size
    first = angle_table(iota(RADIX), outer_index, RADIX, -1.0)
    flat = values.reshape(outer_count, inner_size * column_count)
    step_real, step_imag = table_left("ja,an->jn", first, flat, None)
    step_real = step_real.reshape(RADIX, inner_size, column_count)
    step_imag = step_imag.reshape(RADIX, inner_size, column_count)
    twist_cos, twist_sin = angle_table(iota(RADIX), iota(inner_size), length, -1.0)
    step_real, step_imag = lax.optimization_barrier(rotate(
        step_real, step_imag, twist_cos[:, :, None], twist_sin[:, :, None]
    ))
    second = angle_table(iota(inner_size // 2), iota(inner_size), inner_size, -1.0)
    final_real, final_imag = table_left("mb,jbc->mjc", second, step_real, step_imag)
    alternating = (1 - 2 * (iota(inner_size) % 2)).astype(jnp.float32)
    nyquist = contract("b,bc->c", alternating, step_real[0])
    final_imag = final_imag.at[0, 0].set(nyquist)
    return final_real, final_imag


def column_part(real_part, imag_part, length, sense_sign, offset):
    outer_count, part_size, column_count = real_part.shape
    inner_size = length // RADIX
    first = angle_table(iota(RADIX), iota(outer_count), RADIX, sense_sign)
    flat_real = real_part.reshape(outer_count, part_size * column_count)
    flat_imag = imag_part.reshape(outer_count, part_size * column_count)
    step_real, step_imag = table_left("ja,an->jn", first, flat_real, flat_imag)
    step_real = step_real.reshape(RADIX, part_size, column_count)
    step_imag = step_imag.reshape(RADIX, part_size, column_count)
    twist_cos, twist_sin = angle_table(iota(RADIX), offset + iota(part_size), length, sense_sign)
    step_real, step_imag = lax.optimization_barrier(rotate(
        step_real, step_imag, twist_cos[:, :, None], twist_sin[:, :, None]
    ))
    second_cos, second_sin = angle_table(iota(inner_size), offset + iota(part_size), inner_size, sense_sign)
    final_real = contract("mb,kbc->mkc", second_cos, step_real) - contract(
        "mb,kbc->mkc", second_sin, step_imag
    )
    return final_real.reshape(length, column_count)


def row_forward(real_part, imag_part, sense_sign):
    source_count, _, column_count = real_part.shape
    length = source_count * column_count
    first = angle_table(iota(source_count), iota(source_count), source_count, sense_sign)
    step_real, step_imag = table_left("us,src->urc", first, real_part, imag_part)
    twist_cos, twist_sin = angle_table(iota(source_count), iota(column_count), length, sense_sign)
    step_real, step_imag = rotate(
        step_real, step_imag, twist_cos[:, None, :], twist_sin[:, None, :]
    )
    second = angle_table(iota(column_count), iota(column_count), column_count, sense_sign)
    return table_right("urc,cv->urv", step_real, step_imag, second, lax.Precision.HIGH)


def row_inverse(real_part, imag_part, sense_sign):
    source_count, _, column_count = real_part.shape
    length = source_count * column_count
    second = angle_table(iota(column_count), iota(column_count), column_count, sense_sign)
    step_real, step_imag = table_right(
        "urv,vc->urc", real_part, imag_part, second, lax.Precision.HIGH
    )
    twist_cos, twist_sin = angle_table(iota(source_count), iota(column_count), length, sense_sign)
    step_real, step_imag = rotate(
        step_real, step_imag, twist_cos[:, None, :], twist_sin[:, None, :]
    )
    first = angle_table(iota(source_count), iota(source_count), source_count, sense_sign)
    return table_left("su,urc->src", first, step_real, step_imag)


def local(
    left_zero_zero,
    left_zero_one,
    left_one_zero,
    left_one_one,
    right_zero_zero,
    right_zero_one,
    right_one_zero,
    right_one_one,
):
    lefts = [[left_zero_zero, left_zero_one], [left_one_zero, left_one_one]]
    rights = [[right_zero_zero, right_zero_one], [right_one_zero, right_one_one]]
    entry_count = lax.axis_size("entry")
    fft_count = lax.axis_size("fft")
    fft_place = lax.axis_index("fft")
    on_first = fft_place == 0
    local_cols = left_zero_zero.shape[1]
    row_count = left_zero_zero.shape[0] * entry_count
    length = 2 * row_count * local_cols * fft_count
    column_count = local_cols * fft_count
    rows_here = 2 * row_count // (2 * fft_count)

    held_k1 = jnp.concatenate(
        [fft_place * rows_here + iota(rows_here), jnp.full((1,), row_count, jnp.int32)]
    )
    source_cols = (iota(fft_count)[:, None] * local_cols + iota(local_cols)[None, :])
    turns = source_cols[:, None, :] * held_k1[None, :, None] % length
    big_angle = turns.astype(jnp.float32) * (2.0 * math.pi / length)
    big_cos, big_sin = lax.optimization_barrier((jnp.cos(big_angle), jnp.sin(big_angle)))

    member_pieces = (
        [
            rights[target % 2][target % 2] if target // 2 == 0 else rights[1 - target % 2][target % 2]
            for target in range(entry_count)
        ],
        [lefts[target // 2][target % 2] for target in range(entry_count)],
    )
    entry_place = lax.axis_index("entry")
    block_rows = left_zero_zero.shape[0]
    block_outer = block_rows // (2 * row_count // RADIX)
    shift_of_slot = iota(row_count // (2 * row_count // RADIX)) // block_outer
    outer_index = ((entry_place - shift_of_slot) % entry_count) * block_outer + (
        iota(row_count // (2 * row_count // RADIX)) % block_outer
    )
    arrivals = []
    for pieces in member_pieces:
        stacked = digits(jnp.stack(pieces))
        blocks = [stacked[entry_place]]
        for shift in range(1, entry_count):
            pairs = [(place, (place + shift) % entry_count) for place in range(entry_count)]
            blocks.append(
                lax.ppermute(stacked[(entry_place + shift) % entry_count], "entry", pairs)
            )
        arrivals.append(jnp.concatenate(blocks, axis=0))
    spectra = []
    for arrived in arrivals:
        half_real, half_imag = column_half(arrived, outer_index)
        payload = jnp.stack([half_real, half_imag], axis=1)
        got = lax.all_to_all(payload, "fft", 0, 0, tiled=True)
        got_real = got[:, 0]
        got_imag = got[:, 1]
        packed = got_imag[:, 0:1]
        nyquist_row = jnp.where(on_first, packed, 0.0)
        got_imag = jnp.concatenate(
            [jnp.where(on_first, 0.0, packed), got_imag[:, 1:], jnp.zeros_like(packed)], axis=1
        )
        got_real = jnp.concatenate([got_real, nyquist_row], axis=1)
        got_real, got_imag = lax.optimization_barrier(
            rotate(got_real, got_imag, big_cos, -big_sin)
        )
        if spectra:
            other, got_real, got_imag = lax.optimization_barrier((other, got_real, got_imag))
        spectra.append(row_forward(got_real, got_imag, -1.0))
        if len(spectra) == 1:
            other = lax.ppermute(
                jnp.stack(spectra[0]), "entry", [(place, place ^ 2) for place in range(entry_count)]
            )

    mine, own = spectra
    sibling = lax.ppermute(jnp.stack(own), "entry", [(place, place ^ 1) for place in range(entry_count)])
    upper = entry_place // 2 == 0
    pair_real = jnp.where(upper, own[0], sibling[0])
    pair_imag = jnp.where(upper, own[1], sibling[1])
    rest_a_real = jnp.where(upper, sibling[0], own[0])
    rest_a_imag = jnp.where(upper, sibling[1], own[1])
    head_real, head_imag = complex_product(pair_real, pair_imag, *mine)
    rest_real, rest_imag = complex_product(rest_a_real, rest_a_imag, other[0], other[1])
    mixed_real = head_real + rest_real
    mixed_imag = head_imag + rest_imag
    part_rows = rows_here // 2
    pieces = (
        (slice(0, part_rows), True),
        (slice(part_rows, rows_here), False),
    )
    values = None
    nyquist = None
    for rows, with_nyquist in pieces:
        part_real = mixed_real[:, rows]
        part_imag = mixed_imag[:, rows]
        part_cos = big_cos[:, rows]
        part_sin = big_sin[:, rows]
        if with_nyquist:
            part_real = jnp.concatenate([part_real, mixed_real[:, rows_here:]], axis=1)
            part_imag = jnp.concatenate([part_imag, mixed_imag[:, rows_here:]], axis=1)
            part_cos = jnp.concatenate([part_cos, big_cos[:, rows_here:]], axis=1)
            part_sin = jnp.concatenate([part_sin, big_sin[:, rows_here:]], axis=1)
        back_real, back_imag = row_inverse(part_real, part_imag, 1.0)
        back_real, back_imag = rotate(back_real, back_imag, part_cos, part_sin)
        if with_nyquist:
            first_imag = jnp.where(on_first, back_real[:, part_rows:], back_imag[:, 0:1])
            back_imag = jnp.concatenate([first_imag, back_imag[:, 1:part_rows]], axis=1)
            back_real = back_real[:, :part_rows]
        payload = jnp.stack([back_real, back_imag], axis=1)
        got = lax.all_to_all(payload, "fft", 0, 0, tiled=True)
        full_real = got[:, 0]
        full_imag = got[:, 1]
        if with_nyquist:
            nyquist = full_imag[0, 0]
            full_real = full_real.at[0, 0].multiply(0.5)
            full_imag = full_imag.at[0, 0].set(0.0)
        part = column_part(full_real, full_imag, 2 * row_count, 1.0, rows.start)
        values = part if values is None else values + part
    alternating = (1 - 2 * (iota(2 * row_count) % 2)).astype(jnp.float32)
    values = 2.0 * values + alternating[:, None] * nyquist[None, :]
    out_scale = 1.0 / (length * math.sqrt(length // 2))
    return (values * out_scale)[None]


def solution(mesh):
    placed = (
        P("entry", "fft"),
        P("entry", "fft"),
        P("entry", "fft"),
        P("entry", "fft"),
        P("entry", "fft"),
        P("entry", "fft"),
        P("entry", "fft"),
        P("entry", "fft"),
    )
    return jax.shard_map(
        local, mesh=mesh, in_specs=placed, out_specs=P("entry", None, "fft"), check_vma=False
    )
```

```python
import math

import jax
import jax.numpy as jnp
from jax import lax
from jax.sharding import PartitionSpec as P

RADIX = 64


exact_precision = lax.Precision.HIGHEST


def contract(pattern, left_op, right_op, precision=exact_precision):
    return jnp.einsum(
        pattern, left_op, right_op, precision=precision, preferred_element_type=jnp.float32
    )


def iota(count):
    return jnp.arange(count, dtype=jnp.int32)


def angle_table(first_part, second_part, length, sense_sign):
    turns = first_part[:, None] * second_part[None, :] % length
    phase_angle = turns.astype(jnp.float32) * (2.0 * math.pi / length)
    return lax.optimization_barrier((jnp.cos(phase_angle), sense_sign * jnp.sin(phase_angle)))


def rotate(real_part, imag_part, cosine, sine):
    return (real_part * cosine - imag_part * sine, real_part * sine + imag_part * cosine)


def complex_product(left_real, left_imag, right_real, right_imag):
    return (
        left_real * right_real - left_imag * right_imag,
        left_real * right_imag + left_imag * right_real,
    )


def table_left(pattern, table, real_part, imag_part):
    cosine, sine = table
    if imag_part is None:
        return contract(pattern, cosine, real_part), contract(pattern, sine, real_part)
    return (
        contract(pattern, cosine, real_part) - contract(pattern, sine, imag_part),
        contract(pattern, sine, real_part) + contract(pattern, cosine, imag_part),
    )


def table_right(pattern, real_part, imag_part, table, precision=exact_precision):
    cosine, sine = table
    return (
        contract(pattern, real_part, cosine, precision)
        - contract(pattern, imag_part, sine, precision),
        contract(pattern, real_part, sine, precision)
        + contract(pattern, imag_part, cosine, precision),
    )


def digits(limbs):
    return (limbs.astype(jnp.float32) - 32768.0) * (1.0 / 32768.0)


def column_half(values, outer_index):
    row_count, column_count = values.shape
    length = 2 * row_count
    inner_size = length // RADIX
    outer_count = row_count // inner_size
    first = angle_table(iota(RADIX), outer_index, RADIX, -1.0)
    flat = values.reshape(outer_count, inner_size * column_count)
    step_real, step_imag = table_left("ja,an->jn", first, flat, None)
    step_real = step_real.reshape(RADIX, inner_size, column_count)
    step_imag = step_imag.reshape(RADIX, inner_size, column_count)
    twist_cos, twist_sin = angle_table(iota(RADIX), iota(inner_size), length, -1.0)
    step_real, step_imag = lax.optimization_barrier(rotate(
        step_real, step_imag, twist_cos[:, :, None], twist_sin[:, :, None]
    ))
    second = angle_table(iota(inner_size // 2), iota(inner_size), inner_size, -1.0)
    final_real, final_imag = table_left("mb,jbc->mjc", second, step_real, step_imag)
    alternating = (1 - 2 * (iota(inner_size) % 2)).astype(jnp.float32)
    nyquist = contract("b,bc->c", alternating, step_real[0])
    final_imag = final_imag.at[0, 0].set(nyquist)
    return final_real, final_imag


def column_part(real_part, imag_part, length, sense_sign, offset):
    outer_count, part_size, column_count = real_part.shape
    inner_size = length // RADIX
    first = angle_table(iota(RADIX), iota(outer_count), RADIX, sense_sign)
    flat_real = real_part.reshape(outer_count, part_size * column_count)
    flat_imag = imag_part.reshape(outer_count, part_size * column_count)
    step_real, step_imag = table_left("ja,an->jn", first, flat_real, flat_imag)
    step_real = step_real.reshape(RADIX, part_size, column_count)
    step_imag = step_imag.reshape(RADIX, part_size, column_count)
    twist_cos, twist_sin = angle_table(iota(RADIX), offset + iota(part_size), length, sense_sign)
    step_real, step_imag = lax.optimization_barrier(rotate(
        step_real, step_imag, twist_cos[:, :, None], twist_sin[:, :, None]
    ))
    second_cos, second_sin = angle_table(iota(inner_size), offset + iota(part_size), inner_size, sense_sign)
    final_real = contract("mb,kbc->mkc", second_cos, step_real) - contract(
        "mb,kbc->mkc", second_sin, step_imag
    )
    return final_real.reshape(length, column_count)


def row_forward(real_part, imag_part, sense_sign):
    source_count, _, column_count = real_part.shape
    length = source_count * column_count
    first = angle_table(iota(source_count), iota(source_count), source_count, sense_sign)
    step_real, step_imag = table_left("us,src->urc", first, real_part, imag_part)
    twist_cos, twist_sin = angle_table(iota(source_count), iota(column_count), length, sense_sign)
    step_real, step_imag = rotate(
        step_real, step_imag, twist_cos[:, None, :], twist_sin[:, None, :]
    )
    second = angle_table(iota(column_count), iota(column_count), column_count, sense_sign)
    return table_right("urc,cv->urv", step_real, step_imag, second, lax.Precision.HIGH)


def row_inverse(real_part, imag_part, sense_sign):
    source_count, _, column_count = real_part.shape
    length = source_count * column_count
    second = angle_table(iota(column_count), iota(column_count), column_count, sense_sign)
    step_real, step_imag = table_right(
        "urv,vc->urc", real_part, imag_part, second, lax.Precision.HIGH
    )
    twist_cos, twist_sin = angle_table(iota(source_count), iota(column_count), length, sense_sign)
    step_real, step_imag = rotate(
        step_real, step_imag, twist_cos[:, None, :], twist_sin[:, None, :]
    )
    first = angle_table(iota(source_count), iota(source_count), source_count, sense_sign)
    return table_left("su,urc->src", first, step_real, step_imag)


def local(
    left_zero_zero,
    left_zero_one,
    left_one_zero,
    left_one_one,
    right_zero_zero,
    right_zero_one,
    right_one_zero,
    right_one_one,
):
    lefts = [[left_zero_zero, left_zero_one], [left_one_zero, left_one_one]]
    rights = [[right_zero_zero, right_zero_one], [right_one_zero, right_one_one]]
    entry_count = lax.axis_size("entry")
    fft_count = lax.axis_size("fft")
    fft_place = lax.axis_index("fft")
    on_first = fft_place == 0
    local_cols = left_zero_zero.shape[1]
    row_count = left_zero_zero.shape[0] * entry_count
    length = 2 * row_count * local_cols * fft_count
    column_count = local_cols * fft_count
    rows_here = 2 * row_count // (2 * fft_count)

    held_k1 = jnp.concatenate(
        [fft_place * rows_here + iota(rows_here), jnp.full((1,), row_count, jnp.int32)]
    )
    source_cols = (iota(fft_count)[:, None] * local_cols + iota(local_cols)[None, :])
    turns = source_cols[:, None, :] * held_k1[None, :, None] % length
    big_angle = turns.astype(jnp.float32) * (2.0 * math.pi / length)
    big_cos, big_sin = lax.optimization_barrier((jnp.cos(big_angle), jnp.sin(big_angle)))

    member_pieces = (
        [
            rights[target % 2][target % 2] if target // 2 == 0 else rights[1 - target % 2][target % 2]
            for target in range(entry_count)
        ],
        [lefts[target // 2][target % 2] for target in range(entry_count)],
    )
    entry_place = lax.axis_index("entry")
    block_rows = left_zero_zero.shape[0]
    block_outer = block_rows // (2 * row_count // RADIX)
    shift_of_slot = iota(row_count // (2 * row_count // RADIX)) // block_outer
    outer_index = ((entry_place - shift_of_slot) % entry_count) * block_outer + (
        iota(row_count // (2 * row_count // RADIX)) % block_outer
    )
    arrivals = []
    for pieces in member_pieces:
        stacked = digits(jnp.stack(pieces))
        blocks = [stacked[entry_place]]
        for shift in range(1, entry_count):
            pairs = [(place, (place + shift) % entry_count) for place in range(entry_count)]
            blocks.append(
                lax.ppermute(stacked[(entry_place + shift) % entry_count], "entry", pairs)
            )
        arrivals.append(blocks)
    spectra = []
    for member in range(len(arrivals)):
        half_real, half_imag = column_half(jnp.concatenate(arrivals[member], axis=0), outer_index)
        payload = jnp.stack([half_real, half_imag], axis=1)
        if member + 1 < len(arrivals):
            payload, arrivals[member + 1] = lax.optimization_barrier((payload, arrivals[member + 1]))
        got = lax.all_to_all(payload, "fft", 0, 0, tiled=True)
        got_real = got[:, 0]
        got_imag = got[:, 1]
        packed = got_imag[:, 0:1]
        nyquist_row = jnp.where(on_first, packed, 0.0)
        got_imag = jnp.concatenate(
            [jnp.where(on_first, 0.0, packed), got_imag[:, 1:], jnp.zeros_like(packed)], axis=1
        )
        got_real = jnp.concatenate([got_real, nyquist_row], axis=1)
        got_real, got_imag = lax.optimization_barrier(
            rotate(got_real, got_imag, big_cos, -big_sin)
        )
        if spectra:
            other, got_real, got_imag = lax.optimization_barrier((other, got_real, got_imag))
        spectra.append(row_forward(got_real, got_imag, -1.0))
        if len(spectra) == 1:
            other = lax.ppermute(
                jnp.stack(spectra[0]), "entry", [(place, place ^ 2) for place in range(entry_count)]
            )

    mine, own = spectra
    sibling = lax.ppermute(jnp.stack(own), "entry", [(place, place ^ 1) for place in range(entry_count)])
    upper = entry_place // 2 == 0
    pair_real = jnp.where(upper, own[0], sibling[0])
    pair_imag = jnp.where(upper, own[1], sibling[1])
    rest_a_real = jnp.where(upper, sibling[0], own[0])
    rest_a_imag = jnp.where(upper, sibling[1], own[1])
    head_real, head_imag = complex_product(pair_real, pair_imag, *mine)
    rest_real, rest_imag = complex_product(rest_a_real, rest_a_imag, other[0], other[1])
    mixed_real = head_real + rest_real
    mixed_imag = head_imag + rest_imag
    part_rows = rows_here // 2
    pieces = (
        (slice(0, part_rows), True),
        (slice(part_rows, rows_here), False),
    )
    values = None
    nyquist = None
    for rows, with_nyquist in pieces:
        part_real = mixed_real[:, rows]
        part_imag = mixed_imag[:, rows]
        part_cos = big_cos[:, rows]
        part_sin = big_sin[:, rows]
        if with_nyquist:
            part_real = jnp.concatenate([part_real, mixed_real[:, rows_here:]], axis=1)
            part_imag = jnp.concatenate([part_imag, mixed_imag[:, rows_here:]], axis=1)
            part_cos = jnp.concatenate([part_cos, big_cos[:, rows_here:]], axis=1)
            part_sin = jnp.concatenate([part_sin, big_sin[:, rows_here:]], axis=1)
        back_real, back_imag = row_inverse(part_real, part_imag, 1.0)
        back_real, back_imag = rotate(back_real, back_imag, part_cos, part_sin)
        if with_nyquist:
            first_imag = jnp.where(on_first, back_real[:, part_rows:], back_imag[:, 0:1])
            back_imag = jnp.concatenate([first_imag, back_imag[:, 1:part_rows]], axis=1)
            back_real = back_real[:, :part_rows]
        payload = jnp.stack([back_real, back_imag], axis=1)
        got = lax.all_to_all(payload, "fft", 0, 0, tiled=True)
        full_real = got[:, 0]
        full_imag = got[:, 1]
        if with_nyquist:
            nyquist = full_imag[0, 0]
            full_real = full_real.at[0, 0].multiply(0.5)
            full_imag = full_imag.at[0, 0].set(0.0)
        part = column_part(full_real, full_imag, 2 * row_count, 1.0, rows.start)
        values = part if values is None else values + part
    alternating = (1 - 2 * (iota(2 * row_count) % 2)).astype(jnp.float32)
    values = 2.0 * values + alternating[:, None] * nyquist[None, :]
    out_scale = 1.0 / (length * math.sqrt(length // 2))
    return (values * out_scale)[None]


def solution(mesh):
    placed = (
        P("entry", "fft"),
        P("entry", "fft"),
        P("entry", "fft"),
        P("entry", "fft"),
        P("entry", "fft"),
        P("entry", "fft"),
        P("entry", "fft"),
        P("entry", "fft"),
    )
    return jax.shard_map(
        local, mesh=mesh, in_specs=placed, out_specs=P("entry", None, "fft"), check_vma=False
    )
```

```python
import math

import jax
import jax.numpy as jnp
from jax import lax
from jax.sharding import PartitionSpec as P

RADIX = 64


exact_precision = lax.Precision.HIGHEST


def contract(pattern, left_op, right_op, precision=exact_precision):
    return jnp.einsum(
        pattern, left_op, right_op, precision=precision, preferred_element_type=jnp.float32
    )


def iota(count):
    return jnp.arange(count, dtype=jnp.int32)


def angle_table(first_part, second_part, length, sense_sign):
    turns = first_part[:, None] * second_part[None, :] % length
    phase_angle = turns.astype(jnp.float32) * (2.0 * math.pi / length)
    return lax.optimization_barrier((jnp.cos(phase_angle), sense_sign * jnp.sin(phase_angle)))


def rotate(real_part, imag_part, cosine, sine):
    return (real_part * cosine - imag_part * sine, real_part * sine + imag_part * cosine)


def complex_product(left_real, left_imag, right_real, right_imag):
    return (
        left_real * right_real - left_imag * right_imag,
        left_real * right_imag + left_imag * right_real,
    )


def table_left(pattern, table, real_part, imag_part):
    cosine, sine = table
    if imag_part is None:
        return contract(pattern, cosine, real_part), contract(pattern, sine, real_part)
    return (
        contract(pattern, cosine, real_part) - contract(pattern, sine, imag_part),
        contract(pattern, sine, real_part) + contract(pattern, cosine, imag_part),
    )


def table_right(pattern, real_part, imag_part, table, precision=exact_precision):
    cosine, sine = table
    return (
        contract(pattern, real_part, cosine, precision)
        - contract(pattern, imag_part, sine, precision),
        contract(pattern, real_part, sine, precision)
        + contract(pattern, imag_part, cosine, precision),
    )


def digits(limbs):
    return (limbs.astype(jnp.float32) - 32768.0) * (1.0 / 32768.0)


def column_half(values, outer_index):
    row_count, column_count = values.shape
    length = 2 * row_count
    inner_size = length // RADIX
    outer_count = row_count // inner_size
    first = angle_table(iota(RADIX), outer_index, RADIX, -1.0)
    flat = values.reshape(outer_count, inner_size * column_count)
    step_real, step_imag = table_left("ja,an->jn", first, flat, None)
    step_real = step_real.reshape(RADIX, inner_size, column_count)
    step_imag = step_imag.reshape(RADIX, inner_size, column_count)
    twist_cos, twist_sin = angle_table(iota(RADIX), iota(inner_size), length, -1.0)
    step_real, step_imag = lax.optimization_barrier(rotate(
        step_real, step_imag, twist_cos[:, :, None], twist_sin[:, :, None]
    ))
    second = angle_table(iota(inner_size // 2), iota(inner_size), inner_size, -1.0)
    final_real, final_imag = table_left("mb,jbc->mjc", second, step_real, step_imag)
    alternating = (1 - 2 * (iota(inner_size) % 2)).astype(jnp.float32)
    nyquist = contract("b,bc->c", alternating, step_real[0])
    final_imag = final_imag.at[0, 0].set(nyquist)
    return final_real, final_imag


def column_part(real_part, imag_part, length, sense_sign, offset):
    outer_count, part_size, column_count = real_part.shape
    inner_size = length // RADIX
    first = angle_table(iota(RADIX), iota(outer_count), RADIX, sense_sign)
    flat_real = real_part.reshape(outer_count, part_size * column_count)
    flat_imag = imag_part.reshape(outer_count, part_size * column_count)
    step_real, step_imag = table_left("ja,an->jn", first, flat_real, flat_imag)
    step_real = step_real.reshape(RADIX, part_size, column_count)
    step_imag = step_imag.reshape(RADIX, part_size, column_count)
    twist_cos, twist_sin = angle_table(iota(RADIX), offset + iota(part_size), length, sense_sign)
    step_real, step_imag = lax.optimization_barrier(rotate(
        step_real, step_imag, twist_cos[:, :, None], twist_sin[:, :, None]
    ))
    second_cos, second_sin = angle_table(iota(inner_size), offset + iota(part_size), inner_size, sense_sign)
    final_real = contract("mb,kbc->mkc", second_cos, step_real) - contract(
        "mb,kbc->mkc", second_sin, step_imag
    )
    return final_real.reshape(length, column_count)


def row_forward(real_part, imag_part, sense_sign):
    source_count, _, column_count = real_part.shape
    length = source_count * column_count
    first = angle_table(iota(source_count), iota(source_count), source_count, sense_sign)
    step_real, step_imag = table_left("us,src->urc", first, real_part, imag_part)
    twist_cos, twist_sin = angle_table(iota(source_count), iota(column_count), length, sense_sign)
    step_real, step_imag = rotate(
        step_real, step_imag, twist_cos[:, None, :], twist_sin[:, None, :]
    )
    second = angle_table(iota(column_count), iota(column_count), column_count, sense_sign)
    return table_right("urc,cv->urv", step_real, step_imag, second, lax.Precision.HIGH)


def row_inverse(real_part, imag_part, sense_sign):
    source_count, _, column_count = real_part.shape
    length = source_count * column_count
    second = angle_table(iota(column_count), iota(column_count), column_count, sense_sign)
    step_real, step_imag = table_right(
        "urv,vc->urc", real_part, imag_part, second, lax.Precision.HIGH
    )
    twist_cos, twist_sin = angle_table(iota(source_count), iota(column_count), length, sense_sign)
    step_real, step_imag = rotate(
        step_real, step_imag, twist_cos[:, None, :], twist_sin[:, None, :]
    )
    first = angle_table(iota(source_count), iota(source_count), source_count, sense_sign)
    return table_left("su,urc->src", first, step_real, step_imag)


def local(
    left_zero_zero,
    left_zero_one,
    left_one_zero,
    left_one_one,
    right_zero_zero,
    right_zero_one,
    right_one_zero,
    right_one_one,
):
    lefts = [[left_zero_zero, left_zero_one], [left_one_zero, left_one_one]]
    rights = [[right_zero_zero, right_zero_one], [right_one_zero, right_one_one]]
    entry_count = lax.axis_size("entry")
    fft_count = lax.axis_size("fft")
    fft_place = lax.axis_index("fft")
    on_first = fft_place == 0
    local_cols = left_zero_zero.shape[1]
    row_count = left_zero_zero.shape[0] * entry_count
    length = 2 * row_count * local_cols * fft_count
    column_count = local_cols * fft_count
    rows_here = 2 * row_count // (2 * fft_count)

    held_k1 = jnp.concatenate(
        [fft_place * rows_here + iota(rows_here), jnp.full((1,), row_count, jnp.int32)]
    )
    source_cols = (iota(fft_count)[:, None] * local_cols + iota(local_cols)[None, :])
    turns = source_cols[:, None, :] * held_k1[None, :, None] % length
    big_angle = turns.astype(jnp.float32) * (2.0 * math.pi / length)
    big_cos, big_sin = lax.optimization_barrier((jnp.cos(big_angle), jnp.sin(big_angle)))

    member_pieces = (
        [
            rights[target % 2][target % 2] if target // 2 == 0 else rights[1 - target % 2][target % 2]
            for target in range(entry_count)
        ],
        [lefts[target // 2][target % 2] for target in range(entry_count)],
    )
    entry_place = lax.axis_index("entry")
    block_rows = left_zero_zero.shape[0]
    block_outer = block_rows // (2 * row_count // RADIX)
    shift_of_slot = iota(row_count // (2 * row_count // RADIX)) // block_outer
    outer_index = ((entry_place - shift_of_slot) % entry_count) * block_outer + (
        iota(row_count // (2 * row_count // RADIX)) % block_outer
    )
    arrivals = []
    for pieces in member_pieces:
        stacked = digits(jnp.stack(pieces))
        blocks = [stacked[entry_place]]
        for shift in range(1, entry_count):
            pairs = [(place, (place + shift) % entry_count) for place in range(entry_count)]
            blocks.append(
                lax.ppermute(stacked[(entry_place + shift) % entry_count], "entry", pairs)
            )
        arrivals.append(blocks)
    spectra = []
    for member in range(len(arrivals)):
        half_real, half_imag = column_half(jnp.concatenate(arrivals[member], axis=0), outer_index)
        payload = jnp.stack([half_real, half_imag], axis=1)
        if member + 1 < len(arrivals):
            payload, arrivals[member + 1] = lax.optimization_barrier((payload, arrivals[member + 1]))
        got = lax.all_to_all(payload, "fft", 0, 0, tiled=True)
        got_real = got[:, 0]
        got_imag = got[:, 1]
        packed = got_imag[:, 0:1]
        nyquist_row = jnp.where(on_first, packed, 0.0)
        got_imag = jnp.concatenate(
            [jnp.where(on_first, 0.0, packed), got_imag[:, 1:], jnp.zeros_like(packed)], axis=1
        )
        got_real = jnp.concatenate([got_real, nyquist_row], axis=1)
        got_real, got_imag = lax.optimization_barrier(
            rotate(got_real, got_imag, big_cos, -big_sin)
        )
        if spectra:
            other, got_real, got_imag = lax.optimization_barrier((other, got_real, got_imag))
        spectra.append(row_forward(got_real, got_imag, -1.0))
        if len(spectra) == 1:
            other = lax.ppermute(
                tuple(spectra[0]), "entry", [(place, place ^ 2) for place in range(entry_count)]
            )

    mine, own = spectra
    sibling = lax.ppermute(tuple(own), "entry", [(place, place ^ 1) for place in range(entry_count)])
    upper = entry_place // 2 == 0
    pair_real = jnp.where(upper, own[0], sibling[0])
    pair_imag = jnp.where(upper, own[1], sibling[1])
    rest_a_real = jnp.where(upper, sibling[0], own[0])
    rest_a_imag = jnp.where(upper, sibling[1], own[1])
    head_real, head_imag = complex_product(pair_real, pair_imag, *mine)
    rest_real, rest_imag = complex_product(rest_a_real, rest_a_imag, other[0], other[1])
    mixed_real = head_real + rest_real
    mixed_imag = head_imag + rest_imag
    part_rows = rows_here // 2
    pieces = (
        (slice(0, part_rows), True),
        (slice(part_rows, rows_here), False),
    )
    values = None
    nyquist = None
    for rows, with_nyquist in pieces:
        part_real = mixed_real[:, rows]
        part_imag = mixed_imag[:, rows]
        part_cos = big_cos[:, rows]
        part_sin = big_sin[:, rows]
        if with_nyquist:
            part_real = jnp.concatenate([part_real, mixed_real[:, rows_here:]], axis=1)
            part_imag = jnp.concatenate([part_imag, mixed_imag[:, rows_here:]], axis=1)
            part_cos = jnp.concatenate([part_cos, big_cos[:, rows_here:]], axis=1)
            part_sin = jnp.concatenate([part_sin, big_sin[:, rows_here:]], axis=1)
        back_real, back_imag = row_inverse(part_real, part_imag, 1.0)
        back_real, back_imag = rotate(back_real, back_imag, part_cos, part_sin)
        if with_nyquist:
            first_imag = jnp.where(on_first, back_real[:, part_rows:], back_imag[:, 0:1])
            back_imag = jnp.concatenate([first_imag, back_imag[:, 1:part_rows]], axis=1)
            back_real = back_real[:, :part_rows]
        payload = jnp.stack([back_real, back_imag], axis=1)
        got = lax.all_to_all(payload, "fft", 0, 0, tiled=True)
        full_real = got[:, 0]
        full_imag = got[:, 1]
        if with_nyquist:
            nyquist = full_imag[0, 0]
            full_real = full_real.at[0, 0].multiply(0.5)
            full_imag = full_imag.at[0, 0].set(0.0)
        part = column_part(full_real, full_imag, 2 * row_count, 1.0, rows.start)
        values = part if values is None else values + part
    alternating = (1 - 2 * (iota(2 * row_count) % 2)).astype(jnp.float32)
    values = 2.0 * values + alternating[:, None] * nyquist[None, :]
    out_scale = 1.0 / (length * math.sqrt(length // 2))
    return (values * out_scale)[None]


def solution(mesh):
    placed = (
        P("entry", "fft"),
        P("entry", "fft"),
        P("entry", "fft"),
        P("entry", "fft"),
        P("entry", "fft"),
        P("entry", "fft"),
        P("entry", "fft"),
        P("entry", "fft"),
    )
    return jax.shard_map(
        local, mesh=mesh, in_specs=placed, out_specs=P("entry", None, "fft"), check_vma=False
    )
```

```python
import math

import jax
import jax.numpy as jnp
from jax import lax
from jax.sharding import PartitionSpec as P

RADIX = 64


exact_precision = lax.Precision.HIGHEST


def contract(pattern, left_op, right_op, precision=exact_precision):
    return jnp.einsum(
        pattern, left_op, right_op, precision=precision, preferred_element_type=jnp.float32
    )


def iota(count):
    return jnp.arange(count, dtype=jnp.int32)


def angle_table(first_part, second_part, length, sense_sign):
    turns = first_part[:, None] * second_part[None, :] % length
    phase_angle = turns.astype(jnp.float32) * (2.0 * math.pi / length)
    return lax.optimization_barrier((jnp.cos(phase_angle), sense_sign * jnp.sin(phase_angle)))


def rotate(real_part, imag_part, cosine, sine):
    return (real_part * cosine - imag_part * sine, real_part * sine + imag_part * cosine)


def complex_product(left_real, left_imag, right_real, right_imag):
    return (
        left_real * right_real - left_imag * right_imag,
        left_real * right_imag + left_imag * right_real,
    )


def table_left(pattern, table, real_part, imag_part):
    cosine, sine = table
    if imag_part is None:
        return contract(pattern, cosine, real_part), contract(pattern, sine, real_part)
    return (
        contract(pattern, cosine, real_part) - contract(pattern, sine, imag_part),
        contract(pattern, sine, real_part) + contract(pattern, cosine, imag_part),
    )


def table_right(pattern, real_part, imag_part, table, precision=exact_precision):
    cosine, sine = table
    return (
        contract(pattern, real_part, cosine, precision)
        - contract(pattern, imag_part, sine, precision),
        contract(pattern, real_part, sine, precision)
        + contract(pattern, imag_part, cosine, precision),
    )


def digits(limbs):
    return (limbs.astype(jnp.float32) - 32768.0) * (1.0 / 32768.0)


def column_half(values, outer_index):
    row_count, column_count = values.shape
    length = 2 * row_count
    inner_size = length // RADIX
    outer_count = row_count // inner_size
    first = angle_table(iota(RADIX), outer_index, RADIX, -1.0)
    flat = values.reshape(outer_count, inner_size * column_count)
    step_real, step_imag = table_left("ja,an->jn", first, flat, None)
    step_real = step_real.reshape(RADIX, inner_size, column_count)
    step_imag = step_imag.reshape(RADIX, inner_size, column_count)
    twist_cos, twist_sin = angle_table(iota(RADIX), iota(inner_size), length, -1.0)
    step_real, step_imag = lax.optimization_barrier(rotate(
        step_real, step_imag, twist_cos[:, :, None], twist_sin[:, :, None]
    ))
    second = angle_table(iota(inner_size // 2), iota(inner_size), inner_size, -1.0)
    final_real, final_imag = table_left("mb,jbc->mjc", second, step_real, step_imag)
    alternating = (1 - 2 * (iota(inner_size) % 2)).astype(jnp.float32)
    nyquist = contract("b,bc->c", alternating, step_real[0])
    final_imag = final_imag.at[0, 0].set(nyquist)
    return final_real, final_imag


def column_part(real_part, imag_part, length, sense_sign, offset):
    outer_count, part_size, column_count = real_part.shape
    inner_size = length // RADIX
    first = angle_table(iota(RADIX), iota(outer_count), RADIX, sense_sign)
    flat_real = real_part.reshape(outer_count, part_size * column_count)
    flat_imag = imag_part.reshape(outer_count, part_size * column_count)
    step_real, step_imag = table_left("ja,an->jn", first, flat_real, flat_imag)
    step_real = step_real.reshape(RADIX, part_size, column_count)
    step_imag = step_imag.reshape(RADIX, part_size, column_count)
    twist_cos, twist_sin = angle_table(iota(RADIX), offset + iota(part_size), length, sense_sign)
    step_real, step_imag = lax.optimization_barrier(rotate(
        step_real, step_imag, twist_cos[:, :, None], twist_sin[:, :, None]
    ))
    second_cos, second_sin = angle_table(iota(inner_size), offset + iota(part_size), inner_size, sense_sign)
    final_real = contract("mb,kbc->mkc", second_cos, step_real) - contract(
        "mb,kbc->mkc", second_sin, step_imag
    )
    return final_real.reshape(length, column_count)


def row_forward(real_part, imag_part, sense_sign):
    source_count, _, column_count = real_part.shape
    length = source_count * column_count
    first = angle_table(iota(source_count), iota(source_count), source_count, sense_sign)
    step_real, step_imag = table_left("us,src->urc", first, real_part, imag_part)
    twist_cos, twist_sin = angle_table(iota(source_count), iota(column_count), length, sense_sign)
    step_real, step_imag = rotate(
        step_real, step_imag, twist_cos[:, None, :], twist_sin[:, None, :]
    )
    second = angle_table(iota(column_count), iota(column_count), column_count, sense_sign)
    return table_right("urc,cv->urv", step_real, step_imag, second, lax.Precision.HIGH)


def row_inverse(real_part, imag_part, sense_sign):
    source_count, _, column_count = real_part.shape
    length = source_count * column_count
    second = angle_table(iota(column_count), iota(column_count), column_count, sense_sign)
    step_real, step_imag = table_right(
        "urv,vc->urc", real_part, imag_part, second, lax.Precision.HIGH
    )
    twist_cos, twist_sin = angle_table(iota(source_count), iota(column_count), length, sense_sign)
    step_real, step_imag = rotate(
        step_real, step_imag, twist_cos[:, None, :], twist_sin[:, None, :]
    )
    first = angle_table(iota(source_count), iota(source_count), source_count, sense_sign)
    return table_left("su,urc->src", first, step_real, step_imag)


def local(
    left_zero_zero,
    left_zero_one,
    left_one_zero,
    left_one_one,
    right_zero_zero,
    right_zero_one,
    right_one_zero,
    right_one_one,
):
    lefts = [[left_zero_zero, left_zero_one], [left_one_zero, left_one_one]]
    rights = [[right_zero_zero, right_zero_one], [right_one_zero, right_one_one]]
    entry_count = lax.axis_size("entry")
    fft_count = lax.axis_size("fft")
    fft_place = lax.axis_index("fft")
    on_first = fft_place == 0
    local_cols = left_zero_zero.shape[1]
    row_count = left_zero_zero.shape[0] * entry_count
    length = 2 * row_count * local_cols * fft_count
    column_count = local_cols * fft_count
    rows_here = 2 * row_count // (2 * fft_count)

    held_k1 = jnp.concatenate(
        [fft_place * rows_here + iota(rows_here), jnp.full((1,), row_count, jnp.int32)]
    )
    source_cols = (iota(fft_count)[:, None] * local_cols + iota(local_cols)[None, :])
    turns = source_cols[:, None, :] * held_k1[None, :, None] % length
    big_angle = turns.astype(jnp.float32) * (2.0 * math.pi / length)
    big_cos, big_sin = lax.optimization_barrier((jnp.cos(big_angle), jnp.sin(big_angle)))

    member_pieces = (
        [
            rights[target % 2][target % 2] if target // 2 == 0 else rights[1 - target % 2][target % 2]
            for target in range(entry_count)
        ],
        [lefts[target // 2][target % 2] for target in range(entry_count)],
    )
    entry_place = lax.axis_index("entry")
    block_rows = left_zero_zero.shape[0]
    block_outer = block_rows // (2 * row_count // RADIX)
    shift_of_slot = iota(row_count // (2 * row_count // RADIX)) // block_outer
    outer_index = ((entry_place - shift_of_slot) % entry_count) * block_outer + (
        iota(row_count // (2 * row_count // RADIX)) % block_outer
    )
    arrivals = []
    for pieces in member_pieces:
        stacked = digits(jnp.stack(pieces))
        blocks = [stacked[entry_place]]
        for shift in range(1, entry_count):
            pairs = [(place, (place + shift) % entry_count) for place in range(entry_count)]
            blocks.append(
                lax.ppermute(stacked[(entry_place + shift) % entry_count], "entry", pairs)
            )
        arrivals.append(blocks)
    spectra = []
    for member in range(len(arrivals)):
        half_real, half_imag = column_half(jnp.concatenate(arrivals[member], axis=0), outer_index)
        payload = jnp.stack([half_real, half_imag], axis=1)
        if member + 1 < len(arrivals):
            payload, arrivals[member + 1] = lax.optimization_barrier((payload, arrivals[member + 1]))
        got = lax.all_to_all(payload, "fft", 0, 0, tiled=True)
        got_real = got[:, 0]
        got_imag = got[:, 1]
        packed = got_imag[:, 0:1]
        nyquist_row = jnp.where(on_first, packed, 0.0)
        got_imag = jnp.concatenate(
            [jnp.where(on_first, 0.0, packed), got_imag[:, 1:], jnp.zeros_like(packed)], axis=1
        )
        got_real = jnp.concatenate([got_real, nyquist_row], axis=1)
        got_real, got_imag = lax.optimization_barrier(
            rotate(got_real, got_imag, big_cos, -big_sin)
        )
        if spectra:
            other, got_real, got_imag = lax.optimization_barrier((other, got_real, got_imag))
        spectra.append(row_forward(got_real, got_imag, -1.0))
        if len(spectra) == 1:
            other = lax.ppermute(
                jnp.stack(spectra[0]), "entry", [(place, place ^ 2) for place in range(entry_count)]
            )

    mine, own = spectra
    sibling = lax.ppermute(jnp.stack(own), "entry", [(place, place ^ 1) for place in range(entry_count)])
    upper = entry_place // 2 == 0
    pair_real = jnp.where(upper, own[0], sibling[0])
    pair_imag = jnp.where(upper, own[1], sibling[1])
    rest_a_real = jnp.where(upper, sibling[0], own[0])
    rest_a_imag = jnp.where(upper, sibling[1], own[1])
    head_real, head_imag = complex_product(pair_real, pair_imag, *mine)
    rest_real, rest_imag = complex_product(rest_a_real, rest_a_imag, other[0], other[1])
    mixed_real = head_real + rest_real
    mixed_imag = head_imag + rest_imag
    part_rows = rows_here
    pieces = ((slice(0, part_rows), True),)
    values = None
    nyquist = None
    for rows, with_nyquist in pieces:
        part_real = mixed_real[:, rows]
        part_imag = mixed_imag[:, rows]
        part_cos = big_cos[:, rows]
        part_sin = big_sin[:, rows]
        if with_nyquist:
            part_real = jnp.concatenate([part_real, mixed_real[:, rows_here:]], axis=1)
            part_imag = jnp.concatenate([part_imag, mixed_imag[:, rows_here:]], axis=1)
            part_cos = jnp.concatenate([part_cos, big_cos[:, rows_here:]], axis=1)
            part_sin = jnp.concatenate([part_sin, big_sin[:, rows_here:]], axis=1)
        back_real, back_imag = row_inverse(part_real, part_imag, 1.0)
        back_real, back_imag = rotate(back_real, back_imag, part_cos, part_sin)
        if with_nyquist:
            first_imag = jnp.where(on_first, back_real[:, part_rows:], back_imag[:, 0:1])
            back_imag = jnp.concatenate([first_imag, back_imag[:, 1:part_rows]], axis=1)
            back_real = back_real[:, :part_rows]
        payload = jnp.stack([back_real, back_imag], axis=1)
        got = lax.all_to_all(payload, "fft", 0, 0, tiled=True)
        full_real = got[:, 0]
        full_imag = got[:, 1]
        if with_nyquist:
            nyquist = full_imag[0, 0]
            full_real = full_real.at[0, 0].multiply(0.5)
            full_imag = full_imag.at[0, 0].set(0.0)
        part = column_part(full_real, full_imag, 2 * row_count, 1.0, rows.start)
        values = part if values is None else values + part
    alternating = (1 - 2 * (iota(2 * row_count) % 2)).astype(jnp.float32)
    values = 2.0 * values + alternating[:, None] * nyquist[None, :]
    out_scale = 1.0 / (length * math.sqrt(length // 2))
    return (values * out_scale)[None]


def solution(mesh):
    placed = (
        P("entry", "fft"),
        P("entry", "fft"),
        P("entry", "fft"),
        P("entry", "fft"),
        P("entry", "fft"),
        P("entry", "fft"),
        P("entry", "fft"),
        P("entry", "fft"),
    )
    return jax.shard_map(
        local, mesh=mesh, in_specs=placed, out_specs=P("entry", None, "fft"), check_vma=False
    )
```

```python
import math

import jax
import jax.numpy as jnp
from jax import lax
from jax.sharding import PartitionSpec as P

RADIX = 64


exact_precision = lax.Precision.HIGHEST


def contract(pattern, left_op, right_op, precision=exact_precision):
    return jnp.einsum(
        pattern, left_op, right_op, precision=precision, preferred_element_type=jnp.float32
    )


def iota(count):
    return jnp.arange(count, dtype=jnp.int32)


def angle_table(first_part, second_part, length, sense_sign):
    turns = first_part[:, None] * second_part[None, :] % length
    phase_angle = turns.astype(jnp.float32) * (2.0 * math.pi / length)
    return lax.optimization_barrier((jnp.cos(phase_angle), sense_sign * jnp.sin(phase_angle)))


def rotate(real_part, imag_part, cosine, sine):
    return (real_part * cosine - imag_part * sine, real_part * sine + imag_part * cosine)


def complex_product(left_real, left_imag, right_real, right_imag):
    return (
        left_real * right_real - left_imag * right_imag,
        left_real * right_imag + left_imag * right_real,
    )


def table_left(pattern, table, real_part, imag_part, precision=exact_precision):
    cosine, sine = table
    if imag_part is None:
        return (
            contract(pattern, cosine, real_part, precision),
            contract(pattern, sine, real_part, precision),
        )
    return (
        contract(pattern, cosine, real_part, precision)
        - contract(pattern, sine, imag_part, precision),
        contract(pattern, sine, real_part, precision)
        + contract(pattern, cosine, imag_part, precision),
    )


def table_right(pattern, real_part, imag_part, table, precision=exact_precision):
    cosine, sine = table
    return (
        contract(pattern, real_part, cosine, precision)
        - contract(pattern, imag_part, sine, precision),
        contract(pattern, real_part, sine, precision)
        + contract(pattern, imag_part, cosine, precision),
    )


def digits(limbs):
    return (limbs.astype(jnp.float32) - 32768.0) * (1.0 / 32768.0)


def column_half(values, outer_index):
    row_count, column_count = values.shape
    length = 2 * row_count
    inner_size = length // RADIX
    outer_count = row_count // inner_size
    first = angle_table(iota(RADIX), outer_index, RADIX, -1.0)
    flat = values.reshape(outer_count, inner_size * column_count)
    step_real, step_imag = table_left("ja,an->jn", first, flat, None)
    step_real = step_real.reshape(RADIX, inner_size, column_count)
    step_imag = step_imag.reshape(RADIX, inner_size, column_count)
    twist_cos, twist_sin = angle_table(iota(RADIX), iota(inner_size), length, -1.0)
    step_real, step_imag = lax.optimization_barrier(rotate(
        step_real, step_imag, twist_cos[:, :, None], twist_sin[:, :, None]
    ))
    second = angle_table(iota(inner_size // 2), iota(inner_size), inner_size, -1.0)
    final_real, final_imag = table_left("mb,jbc->mjc", second, step_real, step_imag)
    alternating = (1 - 2 * (iota(inner_size) % 2)).astype(jnp.float32)
    nyquist = contract("b,bc->c", alternating, step_real[0])
    final_imag = final_imag.at[0, 0].set(nyquist)
    return final_real, final_imag


def column_part(real_part, imag_part, length, sense_sign, offset):
    outer_count, part_size, column_count = real_part.shape
    inner_size = length // RADIX
    first = angle_table(iota(RADIX), iota(outer_count), RADIX, sense_sign)
    flat_real = real_part.reshape(outer_count, part_size * column_count)
    flat_imag = imag_part.reshape(outer_count, part_size * column_count)
    step_real, step_imag = table_left("ja,an->jn", first, flat_real, flat_imag)
    step_real = step_real.reshape(RADIX, part_size, column_count)
    step_imag = step_imag.reshape(RADIX, part_size, column_count)
    twist_cos, twist_sin = angle_table(iota(RADIX), offset + iota(part_size), length, sense_sign)
    step_real, step_imag = lax.optimization_barrier(rotate(
        step_real, step_imag, twist_cos[:, :, None], twist_sin[:, :, None]
    ))
    second_cos, second_sin = angle_table(iota(inner_size), offset + iota(part_size), inner_size, sense_sign)
    final_real = contract("mb,kbc->mkc", second_cos, step_real) - contract(
        "mb,kbc->mkc", second_sin, step_imag
    )
    return final_real.reshape(length, column_count)


def row_forward(real_part, imag_part, sense_sign):
    source_count, _, column_count = real_part.shape
    length = source_count * column_count
    first = angle_table(iota(source_count), iota(source_count), source_count, sense_sign)
    step_real, step_imag = table_left(
        "us,src->urc", first, real_part, imag_part, lax.Precision.HIGH
    )
    twist_cos, twist_sin = angle_table(iota(source_count), iota(column_count), length, sense_sign)
    step_real, step_imag = rotate(
        step_real, step_imag, twist_cos[:, None, :], twist_sin[:, None, :]
    )
    second = angle_table(iota(column_count), iota(column_count), column_count, sense_sign)
    return table_right("urc,cv->urv", step_real, step_imag, second, lax.Precision.HIGH)


def row_inverse(real_part, imag_part, sense_sign):
    source_count, _, column_count = real_part.shape
    length = source_count * column_count
    second = angle_table(iota(column_count), iota(column_count), column_count, sense_sign)
    step_real, step_imag = table_right(
        "urv,vc->urc", real_part, imag_part, second, lax.Precision.HIGH
    )
    twist_cos, twist_sin = angle_table(iota(source_count), iota(column_count), length, sense_sign)
    step_real, step_imag = rotate(
        step_real, step_imag, twist_cos[:, None, :], twist_sin[:, None, :]
    )
    first = angle_table(iota(source_count), iota(source_count), source_count, sense_sign)
    return table_left("su,urc->src", first, step_real, step_imag)


def local(
    left_zero_zero,
    left_zero_one,
    left_one_zero,
    left_one_one,
    right_zero_zero,
    right_zero_one,
    right_one_zero,
    right_one_one,
):
    lefts = [[left_zero_zero, left_zero_one], [left_one_zero, left_one_one]]
    rights = [[right_zero_zero, right_zero_one], [right_one_zero, right_one_one]]
    entry_count = lax.axis_size("entry")
    fft_count = lax.axis_size("fft")
    fft_place = lax.axis_index("fft")
    on_first = fft_place == 0
    local_cols = left_zero_zero.shape[1]
    row_count = left_zero_zero.shape[0] * entry_count
    length = 2 * row_count * local_cols * fft_count
    column_count = local_cols * fft_count
    rows_here = 2 * row_count // (2 * fft_count)

    held_k1 = jnp.concatenate(
        [fft_place * rows_here + iota(rows_here), jnp.full((1,), row_count, jnp.int32)]
    )
    source_cols = (iota(fft_count)[:, None] * local_cols + iota(local_cols)[None, :])
    turns = source_cols[:, None, :] * held_k1[None, :, None] % length
    big_angle = turns.astype(jnp.float32) * (2.0 * math.pi / length)
    big_cos, big_sin = lax.optimization_barrier((jnp.cos(big_angle), jnp.sin(big_angle)))

    member_pieces = (
        [
            rights[target % 2][target % 2] if target // 2 == 0 else rights[1 - target % 2][target % 2]
            for target in range(entry_count)
        ],
        [lefts[target // 2][target % 2] for target in range(entry_count)],
    )
    entry_place = lax.axis_index("entry")
    block_rows = left_zero_zero.shape[0]
    block_outer = block_rows // (2 * row_count // RADIX)
    shift_of_slot = iota(row_count // (2 * row_count // RADIX)) // block_outer
    outer_index = ((entry_place - shift_of_slot) % entry_count) * block_outer + (
        iota(row_count // (2 * row_count // RADIX)) % block_outer
    )
    arrivals = []
    for pieces in member_pieces:
        stacked = digits(jnp.stack(pieces))
        blocks = [stacked[entry_place]]
        for shift in range(1, entry_count):
            pairs = [(place, (place + shift) % entry_count) for place in range(entry_count)]
            blocks.append(
                lax.ppermute(stacked[(entry_place + shift) % entry_count], "entry", pairs)
            )
        arrivals.append(blocks)
    spectra = []
    for member in range(len(arrivals)):
        half_real, half_imag = column_half(jnp.concatenate(arrivals[member], axis=0), outer_index)
        payload = jnp.stack([half_real, half_imag], axis=1)
        if member + 1 < len(arrivals):
            payload, arrivals[member + 1] = lax.optimization_barrier((payload, arrivals[member + 1]))
        got = lax.all_to_all(payload, "fft", 0, 0, tiled=True)
        got_real = got[:, 0]
        got_imag = got[:, 1]
        packed = got_imag[:, 0:1]
        nyquist_row = jnp.where(on_first, packed, 0.0)
        got_imag = jnp.concatenate(
            [jnp.where(on_first, 0.0, packed), got_imag[:, 1:], jnp.zeros_like(packed)], axis=1
        )
        got_real = jnp.concatenate([got_real, nyquist_row], axis=1)
        got_real, got_imag = lax.optimization_barrier(
            rotate(got_real, got_imag, big_cos, -big_sin)
        )
        if spectra:
            other, got_real, got_imag = lax.optimization_barrier((other, got_real, got_imag))
        spectra.append(row_forward(got_real, got_imag, -1.0))
        if len(spectra) == 1:
            other = lax.ppermute(
                jnp.stack(spectra[0]), "entry", [(place, place ^ 2) for place in range(entry_count)]
            )

    mine, own = spectra
    sibling = lax.ppermute(jnp.stack(own), "entry", [(place, place ^ 1) for place in range(entry_count)])
    upper = entry_place // 2 == 0
    pair_real = jnp.where(upper, own[0], sibling[0])
    pair_imag = jnp.where(upper, own[1], sibling[1])
    rest_a_real = jnp.where(upper, sibling[0], own[0])
    rest_a_imag = jnp.where(upper, sibling[1], own[1])
    head_real, head_imag = complex_product(pair_real, pair_imag, *mine)
    rest_real, rest_imag = complex_product(rest_a_real, rest_a_imag, other[0], other[1])
    mixed_real = head_real + rest_real
    mixed_imag = head_imag + rest_imag
    part_rows = rows_here
    pieces = ((slice(0, part_rows), True),)
    values = None
    nyquist = None
    for rows, with_nyquist in pieces:
        part_real = mixed_real[:, rows]
        part_imag = mixed_imag[:, rows]
        part_cos = big_cos[:, rows]
        part_sin = big_sin[:, rows]
        if with_nyquist:
            part_real = jnp.concatenate([part_real, mixed_real[:, rows_here:]], axis=1)
            part_imag = jnp.concatenate([part_imag, mixed_imag[:, rows_here:]], axis=1)
            part_cos = jnp.concatenate([part_cos, big_cos[:, rows_here:]], axis=1)
            part_sin = jnp.concatenate([part_sin, big_sin[:, rows_here:]], axis=1)
        back_real, back_imag = row_inverse(part_real, part_imag, 1.0)
        back_real, back_imag = rotate(back_real, back_imag, part_cos, part_sin)
        if with_nyquist:
            first_imag = jnp.where(on_first, back_real[:, part_rows:], back_imag[:, 0:1])
            back_imag = jnp.concatenate([first_imag, back_imag[:, 1:part_rows]], axis=1)
            back_real = back_real[:, :part_rows]
        payload = jnp.stack([back_real, back_imag], axis=1)
        got = lax.all_to_all(payload, "fft", 0, 0, tiled=True)
        full_real = got[:, 0]
        full_imag = got[:, 1]
        if with_nyquist:
            nyquist = full_imag[0, 0]
            full_real = full_real.at[0, 0].multiply(0.5)
            full_imag = full_imag.at[0, 0].set(0.0)
        part = column_part(full_real, full_imag, 2 * row_count, 1.0, rows.start)
        values = part if values is None else values + part
    alternating = (1 - 2 * (iota(2 * row_count) % 2)).astype(jnp.float32)
    values = 2.0 * values + alternating[:, None] * nyquist[None, :]
    out_scale = 1.0 / (length * math.sqrt(length // 2))
    return (values * out_scale)[None]


def solution(mesh):
    placed = (
        P("entry", "fft"),
        P("entry", "fft"),
        P("entry", "fft"),
        P("entry", "fft"),
        P("entry", "fft"),
        P("entry", "fft"),
        P("entry", "fft"),
        P("entry", "fft"),
    )
    return jax.shard_map(
        local, mesh=mesh, in_specs=placed, out_specs=P("entry", None, "fft"), check_vma=False
    )
```

```python
import math

import jax
import jax.numpy as jnp
from jax import lax
from jax.sharding import PartitionSpec as P

RADIX = 64


exact_precision = lax.Precision.HIGHEST


def contract(pattern, left_op, right_op, precision=exact_precision):
    return jnp.einsum(
        pattern, left_op, right_op, precision=precision, preferred_element_type=jnp.float32
    )


def iota(count):
    return jnp.arange(count, dtype=jnp.int32)


def angle_table(first_part, second_part, length, sense_sign):
    turns = first_part[:, None] * second_part[None, :] % length
    phase_angle = turns.astype(jnp.float32) * (2.0 * math.pi / length)
    return lax.optimization_barrier((jnp.cos(phase_angle), sense_sign * jnp.sin(phase_angle)))


def rotate(real_part, imag_part, cosine, sine):
    return (real_part * cosine - imag_part * sine, real_part * sine + imag_part * cosine)


def complex_product(left_real, left_imag, right_real, right_imag):
    return (
        left_real * right_real - left_imag * right_imag,
        left_real * right_imag + left_imag * right_real,
    )


def table_left(pattern, table, real_part, imag_part):
    cosine, sine = table
    if imag_part is None:
        return contract(pattern, cosine, real_part), contract(pattern, sine, real_part)
    return (
        contract(pattern, cosine, real_part) - contract(pattern, sine, imag_part),
        contract(pattern, sine, real_part) + contract(pattern, cosine, imag_part),
    )


def table_right(pattern, real_part, imag_part, table, precision=exact_precision):
    cosine, sine = table
    return (
        contract(pattern, real_part, cosine, precision)
        - contract(pattern, imag_part, sine, precision),
        contract(pattern, real_part, sine, precision)
        + contract(pattern, imag_part, cosine, precision),
    )


def digits(limbs):
    return (limbs.astype(jnp.float32) - 32768.0) * (1.0 / 32768.0)


def column_half(values, outer_index):
    row_count, column_count = values.shape
    length = 2 * row_count
    inner_size = length // RADIX
    outer_count = row_count // inner_size
    first = angle_table(iota(RADIX), outer_index, RADIX, -1.0)
    flat = values.reshape(outer_count, inner_size * column_count)
    step_real, step_imag = table_left("ja,an->jn", first, flat, None)
    step_real = step_real.reshape(RADIX, inner_size, column_count)
    step_imag = step_imag.reshape(RADIX, inner_size, column_count)
    twist_cos, twist_sin = angle_table(iota(RADIX), iota(inner_size), length, -1.0)
    step_real, step_imag = lax.optimization_barrier(rotate(
        step_real, step_imag, twist_cos[:, :, None], twist_sin[:, :, None]
    ))
    second = angle_table(iota(inner_size // 2), iota(inner_size), inner_size, -1.0)
    final_real, final_imag = table_left("mb,jbc->mjc", second, step_real, step_imag)
    alternating = (1 - 2 * (iota(inner_size) % 2)).astype(jnp.float32)
    nyquist = contract("b,bc->c", alternating, step_real[0])
    final_imag = final_imag.at[0, 0].set(nyquist)
    return final_real, final_imag


def column_part(real_part, imag_part, length, sense_sign, offset):
    outer_count, part_size, column_count = real_part.shape
    inner_size = length // RADIX
    first = angle_table(iota(RADIX), iota(outer_count), RADIX, sense_sign)
    flat_real = real_part.reshape(outer_count, part_size * column_count)
    flat_imag = imag_part.reshape(outer_count, part_size * column_count)
    step_real, step_imag = table_left("ja,an->jn", first, flat_real, flat_imag)
    step_real = step_real.reshape(RADIX, part_size, column_count)
    step_imag = step_imag.reshape(RADIX, part_size, column_count)
    twist_cos, twist_sin = angle_table(iota(RADIX), offset + iota(part_size), length, sense_sign)
    step_real, step_imag = lax.optimization_barrier(rotate(
        step_real, step_imag, twist_cos[:, :, None], twist_sin[:, :, None]
    ))
    second_cos, second_sin = angle_table(iota(inner_size), offset + iota(part_size), inner_size, sense_sign)
    final_real = contract("mb,kbc->mkc", second_cos, step_real) - contract(
        "mb,kbc->mkc", second_sin, step_imag
    )
    return final_real.reshape(length, column_count)


def row_forward(real_part, imag_part, sense_sign):
    source_count, _, column_count = real_part.shape
    length = source_count * column_count
    first = angle_table(iota(source_count), iota(source_count), source_count, sense_sign)
    step_real, step_imag = table_left("us,src->urc", first, real_part, imag_part)
    twist_cos, twist_sin = angle_table(iota(source_count), iota(column_count), length, sense_sign)
    step_real, step_imag = rotate(
        step_real, step_imag, twist_cos[:, None, :], twist_sin[:, None, :]
    )
    second = angle_table(iota(column_count), iota(column_count), column_count, sense_sign)
    return table_right("urc,cv->urv", step_real, step_imag, second, lax.Precision.HIGH)


def row_inverse(real_part, imag_part, sense_sign):
    source_count, _, column_count = real_part.shape
    length = source_count * column_count
    second = angle_table(iota(column_count), iota(column_count), column_count, sense_sign)
    step_real, step_imag = table_right(
        "urv,vc->urc", real_part, imag_part, second, lax.Precision.HIGH
    )
    twist_cos, twist_sin = angle_table(iota(source_count), iota(column_count), length, sense_sign)
    step_real, step_imag = rotate(
        step_real, step_imag, twist_cos[:, None, :], twist_sin[:, None, :]
    )
    first = angle_table(iota(source_count), iota(source_count), source_count, sense_sign)
    return table_left("su,urc->src", first, step_real, step_imag)


def local(
    left_zero_zero,
    left_zero_one,
    left_one_zero,
    left_one_one,
    right_zero_zero,
    right_zero_one,
    right_one_zero,
    right_one_one,
):
    lefts = [[left_zero_zero, left_zero_one], [left_one_zero, left_one_one]]
    rights = [[right_zero_zero, right_zero_one], [right_one_zero, right_one_one]]
    entry_count = lax.axis_size("entry")
    fft_count = lax.axis_size("fft")
    fft_place = lax.axis_index("fft")
    on_first = fft_place == 0
    local_cols = left_zero_zero.shape[1]
    row_count = left_zero_zero.shape[0] * entry_count
    length = 2 * row_count * local_cols * fft_count
    column_count = local_cols * fft_count
    rows_here = 2 * row_count // (2 * fft_count)

    held_k1 = jnp.concatenate(
        [fft_place * rows_here + iota(rows_here), jnp.full((1,), row_count, jnp.int32)]
    )
    source_cols = (iota(fft_count)[:, None] * local_cols + iota(local_cols)[None, :])
    turns = source_cols[:, None, :] * held_k1[None, :, None] % length
    big_angle = turns.astype(jnp.float32) * (2.0 * math.pi / length)
    big_cos, big_sin = lax.optimization_barrier((jnp.cos(big_angle), jnp.sin(big_angle)))

    member_pieces = (
        [
            rights[target % 2][target % 2] if target // 2 == 0 else rights[1 - target % 2][target % 2]
            for target in range(entry_count)
        ],
        [lefts[target // 2][target % 2] for target in range(entry_count)],
    )
    entry_place = lax.axis_index("entry")
    block_rows = left_zero_zero.shape[0]
    block_outer = block_rows // (2 * row_count // RADIX)
    shift_of_slot = iota(row_count // (2 * row_count // RADIX)) // block_outer
    outer_index = ((entry_place - shift_of_slot) % entry_count) * block_outer + (
        iota(row_count // (2 * row_count // RADIX)) % block_outer
    )
    arrivals = []
    for pieces in member_pieces:
        stacked = digits(jnp.stack(pieces))
        blocks = [stacked[entry_place]]
        for shift in range(1, entry_count):
            pairs = [(place, (place + shift) % entry_count) for place in range(entry_count)]
            blocks.append(
                lax.ppermute(stacked[(entry_place + shift) % entry_count], "entry", pairs)
            )
        arrivals.append(blocks)
    spectra = []
    for member in range(len(arrivals)):
        half_real, half_imag = column_half(jnp.concatenate(arrivals[member], axis=0), outer_index)
        payload = jnp.stack([half_real, half_imag], axis=1)
        if member + 1 < len(arrivals):
            payload, arrivals[member + 1] = lax.optimization_barrier((payload, arrivals[member + 1]))
        got = lax.all_to_all(payload, "fft", 0, 0, tiled=True)
        got_real = got[:, 0]
        got_imag = got[:, 1]
        packed = got_imag[:, 0:1]
        nyquist_row = jnp.where(on_first, packed, 0.0)
        got_imag = jnp.concatenate(
            [jnp.where(on_first, 0.0, packed), got_imag[:, 1:], jnp.zeros_like(packed)], axis=1
        )
        got_real = jnp.concatenate([got_real, nyquist_row], axis=1)
        got_real, got_imag = lax.optimization_barrier(
            rotate(got_real, got_imag, big_cos, -big_sin)
        )
        if spectra:
            other, got_real, got_imag = lax.optimization_barrier((other, got_real, got_imag))
        spectra.append(row_forward(got_real, got_imag, -1.0))
        if len(spectra) == 1:
            mine_real, mine_imag = spectra[0]
            swapped = lax.ppermute(
                (mine_real[:, :rows_here], mine_imag[:, :rows_here],
                 mine_real[:, rows_here:], mine_imag[:, rows_here:]),
                "entry",
                [(place, place ^ 2) for place in range(entry_count)],
            )
            other = (
                jnp.concatenate([swapped[0], swapped[2]], axis=1),
                jnp.concatenate([swapped[1], swapped[3]], axis=1),
            )

    mine, own = spectra
    sibling = lax.ppermute(jnp.stack(own), "entry", [(place, place ^ 1) for place in range(entry_count)])
    upper = entry_place // 2 == 0
    pair_real = jnp.where(upper, own[0], sibling[0])
    pair_imag = jnp.where(upper, own[1], sibling[1])
    rest_a_real = jnp.where(upper, sibling[0], own[0])
    rest_a_imag = jnp.where(upper, sibling[1], own[1])
    head_real, head_imag = complex_product(pair_real, pair_imag, *mine)
    rest_real, rest_imag = complex_product(rest_a_real, rest_a_imag, other[0], other[1])
    mixed_real = head_real + rest_real
    mixed_imag = head_imag + rest_imag
    part_rows = rows_here
    pieces = ((slice(0, part_rows), True),)
    values = None
    nyquist = None
    for rows, with_nyquist in pieces:
        part_real = mixed_real[:, rows]
        part_imag = mixed_imag[:, rows]
        part_cos = big_cos[:, rows]
        part_sin = big_sin[:, rows]
        if with_nyquist:
            part_real = jnp.concatenate([part_real, mixed_real[:, rows_here:]], axis=1)
            part_imag = jnp.concatenate([part_imag, mixed_imag[:, rows_here:]], axis=1)
            part_cos = jnp.concatenate([part_cos, big_cos[:, rows_here:]], axis=1)
            part_sin = jnp.concatenate([part_sin, big_sin[:, rows_here:]], axis=1)
        back_real, back_imag = row_inverse(part_real, part_imag, 1.0)
        back_real, back_imag = rotate(back_real, back_imag, part_cos, part_sin)
        if with_nyquist:
            first_imag = jnp.where(on_first, back_real[:, part_rows:], back_imag[:, 0:1])
            back_imag = jnp.concatenate([first_imag, back_imag[:, 1:part_rows]], axis=1)
            back_real = back_real[:, :part_rows]
        payload = jnp.stack([back_real, back_imag], axis=1)
        got = lax.all_to_all(payload, "fft", 0, 0, tiled=True)
        full_real = got[:, 0]
        full_imag = got[:, 1]
        if with_nyquist:
            nyquist = full_imag[0, 0]
            full_real = full_real.at[0, 0].multiply(0.5)
            full_imag = full_imag.at[0, 0].set(0.0)
        part = column_part(full_real, full_imag, 2 * row_count, 1.0, rows.start)
        values = part if values is None else values + part
    alternating = (1 - 2 * (iota(2 * row_count) % 2)).astype(jnp.float32)
    values = 2.0 * values + alternating[:, None] * nyquist[None, :]
    out_scale = 1.0 / (length * math.sqrt(length // 2))
    return (values * out_scale)[None]


def solution(mesh):
    placed = (
        P("entry", "fft"),
        P("entry", "fft"),
        P("entry", "fft"),
        P("entry", "fft"),
        P("entry", "fft"),
        P("entry", "fft"),
        P("entry", "fft"),
        P("entry", "fft"),
    )
    return jax.shard_map(
        local, mesh=mesh, in_specs=placed, out_specs=P("entry", None, "fft"), check_vma=False
    )
```

```python
import math

import jax
import jax.numpy as jnp
from jax import lax
from jax.sharding import PartitionSpec as P

RADIX = 64


exact_precision = lax.Precision.HIGHEST


def contract(pattern, left_op, right_op, precision=exact_precision):
    return jnp.einsum(
        pattern, left_op, right_op, precision=precision, preferred_element_type=jnp.float32
    )


def iota(count):
    return jnp.arange(count, dtype=jnp.int32)


def angle_table(first_part, second_part, length, sense_sign):
    turns = first_part[:, None] * second_part[None, :] % length
    phase_angle = turns.astype(jnp.float32) * (2.0 * math.pi / length)
    return lax.optimization_barrier((jnp.cos(phase_angle), sense_sign * jnp.sin(phase_angle)))


def rotate(real_part, imag_part, cosine, sine):
    return (real_part * cosine - imag_part * sine, real_part * sine + imag_part * cosine)


def complex_product(left_real, left_imag, right_real, right_imag):
    return (
        left_real * right_real - left_imag * right_imag,
        left_real * right_imag + left_imag * right_real,
    )


def table_left(pattern, table, real_part, imag_part):
    cosine, sine = table
    if imag_part is None:
        return contract(pattern, cosine, real_part), contract(pattern, sine, real_part)
    return (
        contract(pattern, cosine, real_part) - contract(pattern, sine, imag_part),
        contract(pattern, sine, real_part) + contract(pattern, cosine, imag_part),
    )


def table_right(pattern, real_part, imag_part, table, precision=exact_precision):
    cosine, sine = table
    return (
        contract(pattern, real_part, cosine, precision)
        - contract(pattern, imag_part, sine, precision),
        contract(pattern, real_part, sine, precision)
        + contract(pattern, imag_part, cosine, precision),
    )


def digits(limbs):
    return (limbs.astype(jnp.float32) - 32768.0) * (1.0 / 32768.0)


def column_half(values, outer_index):
    row_count, column_count = values.shape
    length = 2 * row_count
    inner_size = length // RADIX
    outer_count = row_count // inner_size
    first = angle_table(iota(RADIX), outer_index, RADIX, -1.0)
    flat = values.reshape(outer_count, inner_size * column_count)
    step_real, step_imag = table_left("ja,an->jn", first, flat, None)
    step_real = step_real.reshape(RADIX, inner_size, column_count)
    step_imag = step_imag.reshape(RADIX, inner_size, column_count)
    twist_cos, twist_sin = angle_table(iota(RADIX), iota(inner_size), length, -1.0)
    step_real, step_imag = lax.optimization_barrier(rotate(
        step_real, step_imag, twist_cos[:, :, None], twist_sin[:, :, None]
    ))
    second = angle_table(iota(inner_size // 2), iota(inner_size), inner_size, -1.0)
    final_real, final_imag = table_left("mb,jbc->mjc", second, step_real, step_imag)
    alternating = (1 - 2 * (iota(inner_size) % 2)).astype(jnp.float32)
    nyquist = contract("b,bc->c", alternating, step_real[0])
    final_imag = final_imag.at[0, 0].set(nyquist)
    return final_real, final_imag


def column_part(real_part, imag_part, length, sense_sign, offset):
    outer_count, part_size, column_count = real_part.shape
    inner_size = length // RADIX
    first = angle_table(iota(RADIX), iota(outer_count), RADIX, sense_sign)
    flat_real = real_part.reshape(outer_count, part_size * column_count)
    flat_imag = imag_part.reshape(outer_count, part_size * column_count)
    step_real, step_imag = table_left("ja,an->jn", first, flat_real, flat_imag)
    step_real = step_real.reshape(RADIX, part_size, column_count)
    step_imag = step_imag.reshape(RADIX, part_size, column_count)
    twist_cos, twist_sin = angle_table(iota(RADIX), offset + iota(part_size), length, sense_sign)
    step_real, step_imag = lax.optimization_barrier(rotate(
        step_real, step_imag, twist_cos[:, :, None], twist_sin[:, :, None]
    ))
    second_cos, second_sin = angle_table(iota(inner_size), offset + iota(part_size), inner_size, sense_sign)
    final_real = contract("mb,kbc->mkc", second_cos, step_real) - contract(
        "mb,kbc->mkc", second_sin, step_imag
    )
    return final_real.reshape(length, column_count)


def row_forward(real_part, imag_part, sense_sign):
    source_count, _, column_count = real_part.shape
    length = source_count * column_count
    first = angle_table(iota(source_count), iota(source_count), source_count, sense_sign)
    step_real, step_imag = table_left("us,src->urc", first, real_part, imag_part)
    twist_cos, twist_sin = angle_table(iota(source_count), iota(column_count), length, sense_sign)
    step_real, step_imag = rotate(
        step_real, step_imag, twist_cos[:, None, :], twist_sin[:, None, :]
    )
    second = angle_table(iota(column_count), iota(column_count), column_count, sense_sign)
    return table_right("urc,cv->urv", step_real, step_imag, second, lax.Precision.HIGH)


def row_inverse(real_part, imag_part, sense_sign):
    source_count, _, column_count = real_part.shape
    length = source_count * column_count
    second = angle_table(iota(column_count), iota(column_count), column_count, sense_sign)
    step_real, step_imag = table_right(
        "urv,vc->urc", real_part, imag_part, second, lax.Precision.HIGH
    )
    twist_cos, twist_sin = angle_table(iota(source_count), iota(column_count), length, sense_sign)
    step_real, step_imag = rotate(
        step_real, step_imag, twist_cos[:, None, :], twist_sin[:, None, :]
    )
    first = angle_table(iota(source_count), iota(source_count), source_count, sense_sign)
    return table_left("su,urc->src", first, step_real, step_imag)


def local(
    left_zero_zero,
    left_zero_one,
    left_one_zero,
    left_one_one,
    right_zero_zero,
    right_zero_one,
    right_one_zero,
    right_one_one,
):
    lefts = [[left_zero_zero, left_zero_one], [left_one_zero, left_one_one]]
    rights = [[right_zero_zero, right_zero_one], [right_one_zero, right_one_one]]
    entry_count = lax.axis_size("entry")
    fft_count = lax.axis_size("fft")
    fft_place = lax.axis_index("fft")
    on_first = fft_place == 0
    local_cols = left_zero_zero.shape[1]
    row_count = left_zero_zero.shape[0] * entry_count
    length = 2 * row_count * local_cols * fft_count
    column_count = local_cols * fft_count
    rows_here = 2 * row_count // (2 * fft_count)

    held_k1 = jnp.concatenate(
        [fft_place * rows_here + iota(rows_here), jnp.full((1,), row_count, jnp.int32)]
    )
    source_cols = (iota(fft_count)[:, None] * local_cols + iota(local_cols)[None, :])
    turns = source_cols[:, None, :] * held_k1[None, :, None] % length
    big_angle = turns.astype(jnp.float32) * (2.0 * math.pi / length)
    big_cos, big_sin = lax.optimization_barrier((jnp.cos(big_angle), jnp.sin(big_angle)))

    member_pieces = (
        [
            rights[target % 2][target % 2] if target // 2 == 0 else rights[1 - target % 2][target % 2]
            for target in range(entry_count)
        ],
        [lefts[target // 2][target % 2] for target in range(entry_count)],
    )
    entry_place = lax.axis_index("entry")
    block_rows = left_zero_zero.shape[0]
    block_outer = block_rows // (2 * row_count // RADIX)
    shift_of_slot = iota(row_count // (2 * row_count // RADIX)) // block_outer
    outer_index = ((entry_place - shift_of_slot) % entry_count) * block_outer + (
        iota(row_count // (2 * row_count // RADIX)) % block_outer
    )
    arrivals = []
    for pieces in member_pieces:
        stacked = digits(jnp.stack(pieces))
        blocks = [stacked[entry_place]]
        for shift in range(1, entry_count):
            pairs = [(place, (place + shift) % entry_count) for place in range(entry_count)]
            blocks.append(
                lax.ppermute(stacked[(entry_place + shift) % entry_count], "entry", pairs)
            )
        arrivals.append(blocks)
    spectra = []
    for member in range(len(arrivals)):
        half_real, half_imag = column_half(jnp.concatenate(arrivals[member], axis=0), outer_index)
        payload = jnp.stack([half_real, half_imag], axis=1)
        if member + 1 < len(arrivals):
            payload, arrivals[member + 1] = lax.optimization_barrier((payload, arrivals[member + 1]))
        got = lax.all_to_all(payload, "fft", 0, 0, tiled=True)
        got_real = got[:, 0]
        got_imag = got[:, 1]
        packed = got_imag[:, 0:1]
        nyquist_row = jnp.where(on_first, packed, 0.0)
        got_imag = jnp.concatenate(
            [jnp.where(on_first, 0.0, packed), got_imag[:, 1:], jnp.zeros_like(packed)], axis=1
        )
        got_real = jnp.concatenate([got_real, nyquist_row], axis=1)
        got_real, got_imag = lax.optimization_barrier(
            rotate(got_real, got_imag, big_cos, -big_sin)
        )
        if spectra:
            other, got_real, got_imag = lax.optimization_barrier((other, got_real, got_imag))
        spectra.append(row_forward(got_real, got_imag, -1.0))
        if len(spectra) == 1:
            mine_real, mine_imag = spectra[0]
            swapped = lax.ppermute(
                (mine_real[:, :rows_here], mine_imag[:, :rows_here],
                 mine_real[:, rows_here:], mine_imag[:, rows_here:]),
                "entry",
                [(place, place ^ 2) for place in range(entry_count)],
            )
            other = (
                jnp.concatenate([swapped[0], swapped[2]], axis=1),
                jnp.concatenate([swapped[1], swapped[3]], axis=1),
            )

    mine, own = spectra
    swapped = lax.ppermute(
        (own[0][:, :rows_here], own[1][:, :rows_here], own[0][:, rows_here:], own[1][:, rows_here:]),
        "entry",
        [(place, place ^ 1) for place in range(entry_count)],
    )
    sibling = (
        jnp.concatenate([swapped[0], swapped[2]], axis=1),
        jnp.concatenate([swapped[1], swapped[3]], axis=1),
    )
    upper = entry_place // 2 == 0
    pair_real = jnp.where(upper, own[0], sibling[0])
    pair_imag = jnp.where(upper, own[1], sibling[1])
    rest_a_real = jnp.where(upper, sibling[0], own[0])
    rest_a_imag = jnp.where(upper, sibling[1], own[1])
    head_real, head_imag = complex_product(pair_real, pair_imag, *mine)
    rest_real, rest_imag = complex_product(rest_a_real, rest_a_imag, other[0], other[1])
    mixed_real = head_real + rest_real
    mixed_imag = head_imag + rest_imag
    part_rows = rows_here
    pieces = ((slice(0, part_rows), True),)
    values = None
    nyquist = None
    for rows, with_nyquist in pieces:
        part_real = mixed_real[:, rows]
        part_imag = mixed_imag[:, rows]
        part_cos = big_cos[:, rows]
        part_sin = big_sin[:, rows]
        if with_nyquist:
            part_real = jnp.concatenate([part_real, mixed_real[:, rows_here:]], axis=1)
            part_imag = jnp.concatenate([part_imag, mixed_imag[:, rows_here:]], axis=1)
            part_cos = jnp.concatenate([part_cos, big_cos[:, rows_here:]], axis=1)
            part_sin = jnp.concatenate([part_sin, big_sin[:, rows_here:]], axis=1)
        back_real, back_imag = row_inverse(part_real, part_imag, 1.0)
        back_real, back_imag = rotate(back_real, back_imag, part_cos, part_sin)
        if with_nyquist:
            first_imag = jnp.where(on_first, back_real[:, part_rows:], back_imag[:, 0:1])
            back_imag = jnp.concatenate([first_imag, back_imag[:, 1:part_rows]], axis=1)
            back_real = back_real[:, :part_rows]
        payload = jnp.stack([back_real, back_imag], axis=1)
        got = lax.all_to_all(payload, "fft", 0, 0, tiled=True)
        full_real = got[:, 0]
        full_imag = got[:, 1]
        if with_nyquist:
            nyquist = full_imag[0, 0]
            full_real = full_real.at[0, 0].multiply(0.5)
            full_imag = full_imag.at[0, 0].set(0.0)
        part = column_part(full_real, full_imag, 2 * row_count, 1.0, rows.start)
        values = part if values is None else values + part
    alternating = (1 - 2 * (iota(2 * row_count) % 2)).astype(jnp.float32)
    values = 2.0 * values + alternating[:, None] * nyquist[None, :]
    out_scale = 1.0 / (length * math.sqrt(length // 2))
    return (values * out_scale)[None]


def solution(mesh):
    placed = (
        P("entry", "fft"),
        P("entry", "fft"),
        P("entry", "fft"),
        P("entry", "fft"),
        P("entry", "fft"),
        P("entry", "fft"),
        P("entry", "fft"),
        P("entry", "fft"),
    )
    return jax.shard_map(
        local, mesh=mesh, in_specs=placed, out_specs=P("entry", None, "fft"), check_vma=False
    )
```
